256 devices in a mesh: dp: 16 (over y, x), expert: 16 (over z, core).
Axes of the slice: x: 4, y: 4, z: 8, core: 2. Of those that a mesh axis runs over, the one named last changes fastest.
Arguments:
- tokens: bfloat16 [32768, 768], P(('dp', 'expert')), may hold values from -24 to 24
- expert_ids: int32 [32768, 2], P(('dp', 'expert')), may hold values from 0 to 15, all different within a row; in each aligned block of 128 rows (0 to 127, 128 to 255, ...) at most 32 rows name the same one
- router: bfloat16 [768, 16], replicated, may hold values from -0.4375 to 0.4375
- weight_in: bfloat16 [16, 768, 3072], P('expert'), may hold values from -0.21875 to 0.21875
- weight_out: bfloat16 [16, 3072, 768], P('expert'), may hold values from -0.4375 to 0.4375
- premises: bfloat16 [2048, 768], P('dp'), may hold values from -6 to 6
- positive: int32 [512], replicated, may hold values from 0 to 2047
- tile_mask: int32 [256, 16], replicated, may hold values 0 or 1
Outputs:
- grad_in: float32 [16, 768, 3072], P('expert', 'dp')
- grad_out: float32 [16, 3072, 768], P('expert', 'dp')
The draws below stay inside these ranges and needn't reach their ends.
Inputs may be any that keep to these rules, and one draw needn't show every extreme that they name: `expert_ids`: among the 128 tokens of one device no expert is named by more than 32 pairs, and one expert is named by exactly 32; the two experts of a token differ.
All inputs are finite; a program needn't handle non-finite values.
Results may differ from the reference program's by a relative error of at most 0.02.
Values may be sent and summed in bfloat16 or wider, within the bound.
No kernel may reach another device: no remote copies, remote signals or barrier semaphores. Data moves between devices by JAX's collectives and lax.ppermute only.
A program may use at most 128 MiB of HBM per device.

```python
import math
import jax
import jax.numpy as jnp
import numpy as np
from jax import lax

D = 768
FF = 3072
LEN = 64
TOK_DEV = 128
PREM_DEV = 128
EXPERTS = 16
CAP = 32
SEQ_DEV = 2
TOKENS = 32768
SEQS = 512
PREMISES = 2048
N_DP = 16
N_EXPERT = 16


def plant(values, key, smallest, high):
    longest = values.shape.index(max(values.shape))
    spots = []
    for shift in (0, 1):
        where = [jax.random.randint(jax.random.fold_in(key, axis), (), 0, length) for axis, length in enumerate(values.shape)]
        where[longest] = (where[longest] + shift) % values.shape[longest]
        spots.append(tuple(where))
    return values.at[spots[0]].set(smallest).at[spots[1]].set(high)


def spiked(entries, rng, source, target, parts, factor):
    def block_of(axis_at):
        return (jnp.arange(entries.shape[axis_at]) // (entries.shape[axis_at] // parts)).reshape((-1,) + (1,) * (entries.ndim - 1 - axis_at))

    first = jax.random.permutation(rng, parts)[block_of(target)]
    other_side = (block_of(target) + parts // 2) % parts
    return jnp.where((block_of(source) == first) | (block_of(source) == other_side), factor * entries, entries)


def levels(key, extent, pieces, least, top_value):
    factor_of = 1.0
    for dim, parts in pieces:
        draws = jax.random.uniform(jax.random.fold_in(jax.random.fold_in(key, 6), dim), (parts,), jnp.float32, least / len(pieces), top_value / len(pieces))
        factor_of = factor_of * jnp.repeat(jnp.exp(draws), extent[dim] // parts).reshape((-1,) + (1,) * (len(extent) - 1 - dim))
    return factor_of


def deal_out(stream_key, own, number, rows, amount, top, reach, skew):
    ranking = jax.random.permutation(stream_key, amount)
    heavy_load, usual = portions_of(amount, rows * top, reach, skew, True), portions_of(amount, rows * top, reach, skew, False)
    places = jnp.arange(amount)

    def named(sizes, offset_by):
        used = int((sizes > 0).sum())
        fixed = max(1, used // 4)
        shifted = fixed + (places - fixed + offset_by * (used - fixed)) % max(1, amount - fixed)
        return jnp.zeros((amount,), jnp.int32).at[ranking[jnp.where(places < fixed, places, shifted)]].set(jnp.asarray(sizes, jnp.int32))

    sizes = jnp.where(number % 4 == 0, named(heavy_load, number // 4), named(usual, number - number // 4 - 1))
    mixed = jax.random.permutation(jax.random.fold_in(own, 3), amount)
    giver, taker = mixed[0:amount // 2 * 2:2], mixed[1:amount // 2 * 2:2]
    margin = jnp.minimum(sizes[giver] - 1, reach - sizes[taker]) // 2
    margin = jnp.where((giver == ranking[0]) | (taker == ranking[0]) | (sizes[taker] == 0), 0, jnp.maximum(margin, 0))
    shifted = jax.random.randint(jax.random.fold_in(own, 4), (amount // 2,), 0, 1 << 20) % (margin + 1)
    sizes = sizes.at[giver].add(-shifted).at[taker].add(shifted)
    labels = jnp.searchsorted(jnp.cumsum(sizes), jnp.arange(rows * top), side="right").astype(jnp.int32)
    table = labels.reshape(top, rows).T
    table = table[jax.random.permutation(jax.random.fold_in(own, 1), rows)]
    offset_by = jax.random.randint(jax.random.fold_in(own, 2), (rows, 1), 0, top)
    return jnp.take_along_axis(table, (jnp.arange(top)[None, :] + offset_by) % top, axis=1)


def portions_of(number_of, total, bound, slope, full):
    loads = [(1 << 20) // math.isqrt(standing ** slope) + 1 for standing in range(1, number_of + 1)]
    largest = bound if full else min(bound, max(-(-total // number_of), total * loads[0] // sum(loads)))
    least = 1 if total - largest >= number_of - 1 else 0
    given, rest = [largest] + [least] * (number_of - 1), total - largest - least * (number_of - 1)
    while rest > 0:
        movable = [i for i in range(1, number_of) if given[i] < largest] or [i for i in range(1, number_of) if given[i] < bound]
        pool, budget = sum([loads[i] for i in movable]), rest
        for i in movable:
            extra = min(bound - given[i], max(1, budget * loads[i] // pool), rest)
            given[i] = given[i] + extra
            rest = rest - extra
    return np.array(given)


def centred(rng, extent, width, most, pieces=(), kind=jnp.bfloat16):
    gain = levels(rng, extent, pieces, -0.22, 0.18) if pieces else 1.0
    entries = jax.random.normal(rng, extent, jnp.float32) * width * gain
    return jnp.minimum(jnp.maximum(entries, -most), most).astype(kind)


def heavy_noise(own_key, extent, scale, bound, split, heavy, held_as=jnp.bfloat16):
    array = scale * jax.random.normal(own_key, extent, jnp.float32)
    if split:
        array = array * levels(own_key, extent, split, -0.22, 0.18)
    return jnp.clip(spiked(array, jax.random.fold_in(own_key, 3), *heavy), -bound, bound).astype(held_as)


def setup_inputs(seed: int = 0) -> dict:
    key_of = jax.random.split(jax.random.key(seed), 9)
    tokens = heavy_noise(key_of[0], (TOKENS, D), 1.0, 24.0, ((0, 256),), (0, 1, 256, 6.0))
    expert_ids_keys = jax.random.split(jax.random.fold_in(key_of[1], 1), TOKENS // TOK_DEV)
    expert_ids_turns = jax.random.permutation(jax.random.fold_in(key_of[1], 3), TOKENS // TOK_DEV)
    expert_ids = jax.vmap(lambda own, number: deal_out(jax.random.fold_in(key_of[1], 2), own, number, TOK_DEV, EXPERTS, 2, CAP, 2))(expert_ids_keys, expert_ids_turns).reshape((TOKENS, 2))
    router = centred(key_of[2], (D, EXPERTS), (D // 4) ** -0.5, 0.4375)
    weight_in = centred(key_of[3], (EXPERTS, D, FF), D ** -0.5, 0.21875, ((0, 16),))
    weight_out = centred(key_of[4], (EXPERTS, FF, D), (FF // 16) ** -0.5, 0.4375, ((0, 16),))
    premises = centred(key_of[5], (PREMISES, D), 1.0, 6.0, ((0, 16),))
    positive = plant(jax.random.randint(key_of[6], (SEQS,), 0, PREMISES), jax.random.fold_in(key_of[6], 1), 0, PREMISES - 1).astype(jnp.int32)
    tile_mask = plant((jax.random.randint(key_of[7], (N_DP * N_EXPERT, N_DP), 0, 2) < 1).astype(jnp.int32), jax.random.fold_in(key_of[7], 1), 0, 1)
    return dict(tokens=tokens, expert_ids=expert_ids, router=router, weight_in=weight_in, weight_out=weight_out, premises=premises, positive=positive, tile_mask=tile_mask)


SCORE_SCALE = 20.0
LOSS_SCALE = 64.0
EPSILON = 1e-06

def gelu_parts(pre_act):
    inner_arg = 0.7978845608028654 * (pre_act + 0.044715 * pre_act * pre_act * pre_act)
    tangent = jnp.tanh(inner_arg)
    gelu_val = 0.5 * pre_act * (1.0 + tangent)
    slope_val = 0.5 * (1.0 + tangent) + 0.5 * pre_act * (1.0 - tangent * tangent) * 0.7978845608028654 * (1.0 + 0.134145 * pre_act * pre_act)
    return (gelu_val, slope_val)

def route_slots(expert_ids, logits, experts, capacity):
    pick_hot = expert_ids[:, :, None] == jnp.arange(experts, dtype=jnp.int32)[None, None, :]
    picked = lax.optimization_barrier(jnp.sum(jnp.where(pick_hot, logits[:, None, :], jnp.zeros((), logits.dtype)), axis=2))
    gate_wts = jax.nn.sigmoid(picked - picked[:, ::-1]).astype(jnp.bfloat16)
    flat_ids = expert_ids.reshape(-1)
    flat_hot = (flat_ids[:, None] == jnp.arange(experts, dtype=jnp.int32)[None, :]).astype(jnp.int32)
    running = jnp.cumsum(flat_hot, axis=0)
    position = lax.optimization_barrier(jnp.sum(running * flat_hot, axis=1)) - 1
    slot_ids = flat_ids * capacity + position
    return (gate_wts, slot_ids.reshape(expert_ids.shape).astype(jnp.int32))

def contrast_terms(query_vec, key_rows, key_scale, open_mask, pos_hot):
    include = jnp.logical_or(open_mask, pos_hot)
    scores = SCORE_SCALE * lax.dot_general(query_vec, key_rows, (((1,), (1,)), ((), ())), preferred_element_type=jnp.float32) * key_scale[None, :]
    exp_scores = jnp.where(include, jnp.exp(scores), jnp.zeros((), scores.dtype))
    partition = lax.optimization_barrier(jnp.sum(exp_scores, axis=1))
    soft_weight = (exp_scores * key_scale[None, :]).astype(jnp.bfloat16)
    weighted_sum = jnp.dot(soft_weight, key_rows, preferred_element_type=jnp.float32)
    pos_scale = lax.optimization_barrier(jnp.sum(jnp.where(pos_hot, key_scale[None, :], jnp.zeros((), key_scale.dtype)), axis=1))
    pos_vec = jnp.dot(pos_hot.astype(jnp.bfloat16), key_rows, preferred_element_type=jnp.float32) * pos_scale[:, None]
    return (weighted_sum, partition, pos_vec)

def settle(partial_sums):
    rounded = lax.optimization_barrier(partial_sums.astype(jnp.bfloat16))
    return lax.optimization_barrier(jnp.sum(rounded.astype(jnp.float32), axis=0))

def reference(tokens, expert_ids, router, weight_in, weight_out, premises, positive, tile_mask):
    device_count = N_DP * N_EXPERT
    model_width = tokens.shape[1]
    logits = jnp.dot(tokens, router, preferred_element_type=jnp.float32)
    gate_wts, slot_ids = jax.vmap(lambda ids_block, logit_block: route_slots(ids_block, logit_block, EXPERTS, CAP))(expert_ids.reshape(device_count, TOK_DEV, 2), logits.reshape(device_count, TOK_DEV, EXPERTS))
    gate_flat = gate_wts.reshape(-1).astype(jnp.float32)
    sentinel = TOKENS * 2
    pair_ids = jnp.arange(sentinel, dtype=jnp.int32).reshape(device_count, TOK_DEV * 2)
    table = jnp.full((device_count, EXPERTS * CAP), sentinel, dtype=jnp.int32)
    dev_rows = jnp.arange(device_count, dtype=jnp.int32)[:, None]
    table = table.at[dev_rows, slot_ids.reshape(device_count, TOK_DEV * 2)].set(pair_ids)
    table = table.reshape(device_count, EXPERTS, CAP)

    def expert_rows(expert):
        chosen = lax.dynamic_index_in_dim(table, expert, 1, keepdims=False).reshape(-1)
        is_valid = chosen < sentinel
        safe_pair = jnp.where(is_valid, chosen, jnp.zeros((), jnp.int32))
        token_idx = (safe_pair // 2).astype(jnp.int32)
        rows_in = jnp.where(is_valid[:, None], tokens[token_idx], jnp.zeros((), jnp.bfloat16))
        weight = jnp.where(is_valid, gate_flat[safe_pair], jnp.zeros((), gate_flat.dtype))
        return (rows_in, token_idx, weight)

    def forward_expert(moe_sum, expert):
        rows_in, token_idx, weight = expert_rows(expert)
        pre_act = jnp.dot(rows_in, weight_in[expert], preferred_element_type=jnp.float32)
        gelu_val, slope_val = gelu_parts(pre_act)
        result = jnp.dot(gelu_val.astype(jnp.bfloat16), weight_out[expert], preferred_element_type=jnp.float32).astype(jnp.bfloat16)
        moe_sum = moe_sum.at[token_idx].add(weight[:, None] * result.astype(jnp.float32))
        return (moe_sum, None)
    moe_sum, unused = lax.scan(forward_expert, jnp.zeros((TOKENS, model_width), jnp.float32), jnp.arange(EXPERTS, dtype=jnp.int32))
    mixed_out = tokens.astype(jnp.float32) + moe_sum
    pooled = lax.optimization_barrier(jnp.sum(mixed_out.reshape(SEQS, LEN, model_width), axis=1)) / LEN
    row_scale = lax.rsqrt(lax.optimization_barrier(jnp.sum(pooled * pooled, axis=1)) + EPSILON)
    unit_vec = pooled * row_scale[:, None]
    query_vec = unit_vec.astype(jnp.bfloat16)
    key_scale = lax.rsqrt(lax.optimization_barrier(jnp.sum(jnp.square(premises.astype(jnp.float32)), axis=1)) + EPSILON)
    key_index = jnp.arange(PREMISES, dtype=jnp.int32)
    seq_device = (jnp.arange(SEQS, dtype=jnp.int32) // SEQ_DEV).astype(jnp.int32)
    key_open = tile_mask[seq_device[:, None], (key_index // PREM_DEV)[None, :]] == 1
    pos_hot = key_index[None, :] == positive[:, None]
    weighted_sum, partition, pos_vec = contrast_terms(query_vec, premises, key_scale, key_open, pos_hot)
    delta_unit = LOSS_SCALE * SCORE_SCALE * (weighted_sum / partition[:, None] - pos_vec)
    delta_pooled = row_scale[:, None] * (delta_unit - unit_vec * lax.optimization_barrier(jnp.sum(unit_vec * delta_unit, axis=1, keepdims=True)))
    delta_mixed = jnp.repeat(delta_pooled / LEN, LEN, axis=0)
    group_rows = N_EXPERT * CAP

    def backward_expert(expert):
        rows_in, token_idx, weight = expert_rows(expert)
        pre_act = jnp.dot(rows_in, weight_in[expert], preferred_element_type=jnp.float32)
        gelu_val, slope_val = gelu_parts(pre_act)
        hidden = gelu_val.astype(jnp.bfloat16)
        grad_rows = (weight[:, None] * delta_mixed[token_idx]).astype(jnp.bfloat16)
        dhidden = jnp.dot(grad_rows, weight_out[expert].T, preferred_element_type=jnp.float32)
        delta_pre = (dhidden * slope_val).astype(jnp.bfloat16)
        part_out = jnp.einsum('grf,grd->gfd', hidden.reshape(N_DP, group_rows, FF).astype(jnp.float32), grad_rows.reshape(N_DP, group_rows, model_width).astype(jnp.float32))
        out_total = settle(part_out)
        part_in = jnp.einsum('grd,grf->gdf', rows_in.reshape(N_DP, group_rows, model_width).astype(jnp.float32), delta_pre.reshape(N_DP, group_rows, FF).astype(jnp.float32))
        in_total = settle(part_in)
        return (in_total, out_total)
    grad_in, grad_out = lax.map(backward_expert, jnp.arange(EXPERTS, dtype=jnp.int32))
    return (grad_in, grad_out)
```

```python
import jax
import jax.numpy as jnp
from jax import lax
from jax.sharding import PartitionSpec as P

LEN = 64


SCORE_SCALE = 20.0
LOSS_SCALE = 64.0
EPSILON = 1e-06
HIGHEST = lax.Precision.HIGHEST


def gelu_parts(pre_act):
    inner_arg = 0.7978845608028654 * (pre_act + 0.044715 * pre_act * pre_act * pre_act)
    tangent = jnp.tanh(inner_arg)
    gelu_val = 0.5 * pre_act * (1.0 + tangent)
    slope_val = 0.5 * (1.0 + tangent) + 0.5 * pre_act * (
        1.0 - tangent * tangent
    ) * 0.7978845608028654 * (1.0 + 0.134145 * pre_act * pre_act)
    return (gelu_val, slope_val)


def route_slots(expert_ids, logits, experts, capacity):
    pick_hot = expert_ids[:, :, None] == jnp.arange(experts, dtype=jnp.int32)[None, None, :]
    picked = jnp.sum(jnp.where(pick_hot, logits[:, None, :], jnp.zeros((), logits.dtype)), axis=2)
    gate_wts = jax.nn.sigmoid(picked - picked[:, ::-1]).astype(jnp.bfloat16)
    flat_ids = expert_ids.reshape(-1)
    flat_hot = (flat_ids[:, None] == jnp.arange(experts, dtype=jnp.int32)[None, :]).astype(
        jnp.int32
    )
    running = jnp.cumsum(flat_hot, axis=0)
    position = jnp.sum(running * flat_hot, axis=1) - 1
    slot_ids = flat_ids * capacity + position
    return (gate_wts, slot_ids.reshape(expert_ids.shape))


def split_dot(a, b, dims):
    a_hi = a.astype(jnp.bfloat16)
    a_lo = (a - a_hi.astype(jnp.float32)).astype(jnp.bfloat16)
    hi = lax.dot_general(a_hi, b, dims, preferred_element_type=jnp.float32)
    lo = lax.dot_general(a_lo, b, dims, preferred_element_type=jnp.float32)
    return hi + lo


def contrast_terms(query_vec, key_rows, key_scale, open_mask, pos_hot):
    include = jnp.logical_or(open_mask, pos_hot)
    scores = (
        SCORE_SCALE
        * lax.dot_general(
            query_vec, key_rows, (((1,), (1,)), ((), ())), preferred_element_type=jnp.float32
        )
        * key_scale[None, :]
    )
    exp_scores = jnp.where(include, jnp.exp(scores), jnp.zeros((), scores.dtype))
    partition = jnp.sum(exp_scores, axis=1)
    soft_weight = (exp_scores * key_scale[None, :]).astype(jnp.bfloat16)
    weighted_sum = jnp.dot(soft_weight, key_rows, preferred_element_type=jnp.float32)
    pos_scale = jnp.sum(
        jnp.where(pos_hot, key_scale[None, :], jnp.zeros((), key_scale.dtype)), axis=1
    )
    pos_vec = (
        jnp.dot(pos_hot.astype(jnp.bfloat16), key_rows, preferred_element_type=jnp.float32)
        * pos_scale[:, None]
    )
    return (weighted_sum, partition, pos_vec)


def on_device(tokens, expert_ids, router, weight_in, weight_out, premises, positive, tile_mask):
    token_count, model_width = tokens.shape
    ffn_width = weight_in.shape[2]
    experts = router.shape[1]
    expert_size = lax.axis_size("expert")
    dp_size = lax.axis_size("dp")
    capacity = 4 * token_count // expert_size
    slot_total = experts * capacity
    seq_count = token_count // LEN
    dp_index = lax.axis_index("dp")
    col_index = lax.axis_index("expert")
    device = dp_index * expert_size + col_index

    logits = jnp.dot(tokens, router, preferred_element_type=jnp.float32)
    gate_wts, slot_ids = route_slots(expert_ids, logits, experts, capacity)
    slot_hot = slot_ids[:, :, None] == jnp.arange(slot_total, dtype=jnp.int32)[None, None, :]
    placing = jnp.sum(slot_hot.astype(jnp.bfloat16), axis=1)
    combine = jnp.sum(
        jnp.where(slot_hot, gate_wts[:, :, None], jnp.zeros((), jnp.bfloat16)), axis=1
    )
    seq_hot = (
        (jnp.arange(token_count, dtype=jnp.int32) // LEN)[:, None]
        == jnp.arange(seq_count, dtype=jnp.int32)[None, :]
    ).astype(jnp.float32)
    slot_meta = lax.dot_general(
        combine.astype(jnp.float32), seq_hot, (((0,), (0,)), ((), ())),
        precision=HIGHEST, preferred_element_type=jnp.float32,
    )
    meta_all = lax.all_gather(slot_meta.reshape(experts, capacity, seq_count), "expert")
    my_meta = lax.dynamic_index_in_dim(meta_all, col_index, 1, keepdims=False)
    same_src = jnp.eye(expert_size, dtype=jnp.float32)
    meta_t = jnp.transpose(my_meta, (2, 0, 1))
    sel_gate = same_src[:, None, :, None] * meta_t[None, :, :, :]
    sel_gate = sel_gate.reshape(expert_size * seq_count, expert_size * capacity)

    outgoing = lax.dot_general(
        placing, tokens, (((0,), (0,)), ((), ())), preferred_element_type=jnp.float32
    ).astype(jnp.bfloat16)
    outgoing = outgoing.reshape(experts, capacity, model_width)
    arrived = lax.all_to_all(outgoing, "expert", split_axis=0, concat_axis=0, tiled=True)
    input_flat = arrived.reshape(expert_size * capacity, model_width)
    pre_act = jnp.dot(input_flat, weight_in[0], preferred_element_type=jnp.float32)
    gelu_val, slope_flat = gelu_parts(pre_act)
    hidden = gelu_val.astype(jnp.bfloat16)
    seq_hidden = jnp.dot(sel_gate.astype(jnp.bfloat16), hidden, preferred_element_type=jnp.float32)
    moe_seq = split_dot(seq_hidden, weight_out[0], (((1,), (0,)), ((), ())))
    moe_mine = lax.psum_scatter(moe_seq, "expert", scatter_dimension=0, tiled=True)

    token_sum = jnp.sum(tokens.astype(jnp.float32).reshape(seq_count, LEN, model_width), axis=1)
    pooled = (token_sum + moe_mine) / LEN
    row_scale = lax.rsqrt(jnp.sum(pooled * pooled, axis=1) + EPSILON)
    unit_vec = pooled * row_scale[:, None]
    query_vec = unit_vec.astype(jnp.bfloat16)
    prem_count = premises.shape[0]
    key_rows = lax.all_gather(premises, "dp", axis=0, tiled=True)
    key_scale = lax.rsqrt(jnp.sum(jnp.square(key_rows.astype(jnp.float32)), axis=1) + EPSILON)
    key_index = jnp.arange(key_rows.shape[0], dtype=jnp.int32)
    own_positive = lax.dynamic_slice_in_dim(positive, device * seq_count, seq_count)
    mask_row = lax.dynamic_index_in_dim(tile_mask, device, 0, keepdims=False)
    key_open = jnp.repeat(mask_row, prem_count) == 1
    weighted_sum, partition, pos_vec = contrast_terms(
        query_vec,
        key_rows,
        key_scale,
        key_open[None, :],
        key_index[None, :] == own_positive[:, None],
    )
    delta_unit = LOSS_SCALE * SCORE_SCALE * (weighted_sum / partition[:, None] - pos_vec)
    delta_pooled = row_scale[:, None] * (
        delta_unit - unit_vec * jnp.sum(unit_vec * delta_unit, axis=1, keepdims=True)
    )
    delta_seq = delta_pooled / LEN
    delta_row = lax.all_gather(delta_seq, "expert", axis=0, tiled=True)

    grad_flat = lax.dot_general(
        sel_gate, delta_row, (((0,), (0,)), ((), ())),
        precision=HIGHEST, preferred_element_type=jnp.float32,
    ).astype(jnp.bfloat16)
    dhidden = lax.dot_general(
        grad_flat, weight_out[0], (((1,), (1,)), ((), ())), preferred_element_type=jnp.float32
    )
    delta_pre = (dhidden * slope_flat).astype(jnp.bfloat16)
    grad_in_term = lax.dot_general(
        input_flat, delta_pre, (((0,), (0,)), ((), ())), preferred_element_type=jnp.float32
    )
    grad_in = lax.psum_scatter(
        grad_in_term[None].astype(jnp.bfloat16), "dp", scatter_dimension=1, tiled=True
    ).astype(jnp.float32)

    block = ffn_width // dp_size
    hidden_blocks = jnp.transpose(
        seq_hidden.reshape(expert_size * seq_count, dp_size, block), (1, 0, 2)
    )
    hidden_cols = lax.all_to_all(hidden_blocks, "dp", split_axis=0, concat_axis=0, tiled=True)
    hidden_cols = hidden_cols.reshape(dp_size * expert_size * seq_count, block)
    delta_all = lax.all_gather(delta_row.astype(jnp.bfloat16), "dp", axis=0, tiled=True)
    grad_out = split_dot(hidden_cols, delta_all, (((0,), (0,)), ((), ())))
    return (grad_in, grad_out[None])


def solution(mesh):
    in_specs = (
        P(("dp", "expert"), None),
        P(("dp", "expert"), None),
        P(),
        P("expert", None, None),
        P("expert", None, None),
        P("dp", None),
        P(),
        P(),
    )
    out_specs = (P("expert", "dp", None), P("expert", "dp", None))
    return jax.shard_map(
        on_device, mesh=mesh, in_specs=in_specs, out_specs=out_specs, check_vma=False
    )
```

```python
import jax
import jax.numpy as jnp
from jax import lax
from jax.sharding import PartitionSpec as P

LEN = 64


SCORE_SCALE = 20.0
LOSS_SCALE = 64.0
EPSILON = 1e-06
HIGHEST = lax.Precision.HIGHEST


def gelu_parts(pre_act):
    inner_arg = 0.7978845608028654 * (pre_act + 0.044715 * pre_act * pre_act * pre_act)
    tangent = jnp.tanh(inner_arg)
    gelu_val = 0.5 * pre_act * (1.0 + tangent)
    slope_val = 0.5 * (1.0 + tangent) + 0.5 * pre_act * (
        1.0 - tangent * tangent
    ) * 0.7978845608028654 * (1.0 + 0.134145 * pre_act * pre_act)
    return (gelu_val, slope_val)


def route_slots(expert_ids, logits, experts, capacity):
    pick_hot = expert_ids[:, :, None] == jnp.arange(experts, dtype=jnp.int32)[None, None, :]
    picked = jnp.sum(jnp.where(pick_hot, logits[:, None, :], jnp.zeros((), logits.dtype)), axis=2)
    gate_wts = jax.nn.sigmoid(picked - picked[:, ::-1]).astype(jnp.bfloat16)
    flat_ids = expert_ids.reshape(-1)
    flat_hot = (flat_ids[:, None] == jnp.arange(experts, dtype=jnp.int32)[None, :]).astype(
        jnp.int32
    )
    running = jnp.cumsum(flat_hot, axis=0)
    position = jnp.sum(running * flat_hot, axis=1) - 1
    slot_ids = flat_ids * capacity + position
    return (gate_wts, slot_ids.reshape(expert_ids.shape))


def split_dot(a, b, dims):
    a_hi = a.astype(jnp.bfloat16)
    a_lo = (a - a_hi.astype(jnp.float32)).astype(jnp.bfloat16)
    hi = lax.dot_general(a_hi, b, dims, preferred_element_type=jnp.float32)
    lo = lax.dot_general(a_lo, b, dims, preferred_element_type=jnp.float32)
    return hi + lo


def contrast_terms(query_vec, key_rows, key_scale, open_mask, pos_hot):
    include = jnp.logical_or(open_mask, pos_hot)
    scores = (
        SCORE_SCALE
        * lax.dot_general(
            query_vec, key_rows, (((1,), (1,)), ((), ())), preferred_element_type=jnp.float32
        )
        * key_scale[None, :]
    )
    exp_scores = jnp.where(include, jnp.exp(scores), jnp.zeros((), scores.dtype))
    partition = jnp.sum(exp_scores, axis=1)
    soft_weight = (exp_scores * key_scale[None, :]).astype(jnp.bfloat16)
    weighted_sum = jnp.dot(soft_weight, key_rows, preferred_element_type=jnp.float32)
    pos_scale = jnp.sum(
        jnp.where(pos_hot, key_scale[None, :], jnp.zeros((), key_scale.dtype)), axis=1
    )
    pos_vec = (
        jnp.dot(pos_hot.astype(jnp.bfloat16), key_rows, preferred_element_type=jnp.float32)
        * pos_scale[:, None]
    )
    return (weighted_sum, partition, pos_vec)


def ring_pairs(nx, ny, along_x, step):
    pairs = []
    for y in range(ny):
        for x in range(nx):
            if along_x:
                pairs.append((y * nx + x, y * nx + (x + step) % nx))
            else:
                pairs.append((y * nx + x, ((y + step) % ny) * nx + x))
    return pairs


def take_chunk(chunks, index, count):
    return lax.dynamic_index_in_dim(chunks, lax.rem(index + 2 * count, count), 0, keepdims=False)


def ring_start(chunks, count, pos):
    half = chunks.shape[-1] // 2
    fwd, bwd = chunks[..., :half], chunks[..., half:]
    return dict(fwd=fwd, bwd=bwd, count=count, pos=pos,
                acc_f=take_chunk(fwd, pos - 1, count).astype(jnp.float32),
                acc_b=take_chunk(bwd, pos + 1, count).astype(jnp.float32))


def ring_step(state, k, fwd_pairs, bwd_pairs):
    count, pos = state["count"], state["pos"]
    got_f = lax.ppermute(state["acc_f"].astype(jnp.bfloat16), "dp", fwd_pairs)
    got_b = lax.ppermute(state["acc_b"].astype(jnp.bfloat16), "dp", bwd_pairs)
    state = dict(state)
    state["acc_f"] = got_f.astype(jnp.float32) + take_chunk(state["fwd"], pos - 2 - k, count).astype(jnp.float32)
    state["acc_b"] = got_b.astype(jnp.float32) + take_chunk(state["bwd"], pos + 2 + k, count).astype(jnp.float32)
    return state


def ring_result(state):
    return jnp.concatenate([state["acc_f"], state["acc_b"]], axis=-1)


def reduce_scatter_2d(partial, nx, ny, x_pos, y_pos):
    rows = partial.shape[0] // (nx * ny)
    width = partial.shape[1]
    half = width // 2
    grid = partial.reshape(ny, nx, rows, width)
    first = jnp.transpose(grid[..., :half], (1, 0, 2, 3))
    second = grid[..., half:]
    x_f, x_b = ring_pairs(nx, ny, True, 1), ring_pairs(nx, ny, True, -1)
    y_f, y_b = ring_pairs(nx, ny, False, 1), ring_pairs(nx, ny, False, -1)
    ra = ring_start(first, nx, x_pos)
    rb = ring_start(second, ny, y_pos)
    for k in range(max(nx, ny) - 1):
        if k < nx - 1:
            ra = ring_step(ra, k, x_f, x_b)
        if k < ny - 1:
            rb = ring_step(rb, k, y_f, y_b)
    ra = ring_start(ring_result(ra), ny, y_pos)
    rb = ring_start(ring_result(rb), nx, x_pos)
    for k in range(max(nx, ny) - 1):
        if k < ny - 1:
            ra = ring_step(ra, k, y_f, y_b)
        if k < nx - 1:
            rb = ring_step(rb, k, x_f, x_b)
    return jnp.concatenate([ring_result(ra), ring_result(rb)], axis=-1)


def on_device(tokens, expert_ids, router, weight_in, weight_out, premises, positive, tile_mask):
    token_count, model_width = tokens.shape
    ffn_width = weight_in.shape[2]
    experts = router.shape[1]
    expert_size = lax.axis_size("expert")
    dp_size = lax.axis_size("dp")
    nx = 4
    ny = dp_size // nx
    capacity = 4 * token_count // expert_size
    slot_total = experts * capacity
    seq_count = token_count // LEN
    row_seqs = expert_size * seq_count
    dp_index = lax.axis_index("dp")
    col_index = lax.axis_index("expert")
    device = dp_index * expert_size + col_index

    logits = jnp.dot(tokens, router, preferred_element_type=jnp.float32)
    gate_wts, slot_ids = route_slots(expert_ids, logits, experts, capacity)
    slot_hot = slot_ids[:, :, None] == jnp.arange(slot_total, dtype=jnp.int32)[None, None, :]
    placing = jnp.sum(slot_hot.astype(jnp.bfloat16), axis=1)
    combine = jnp.sum(
        jnp.where(slot_hot, gate_wts[:, :, None], jnp.zeros((), jnp.bfloat16)), axis=1
    )
    extra = 128
    seq_hot = (
        (jnp.arange(token_count, dtype=jnp.int32) // LEN)[:, None]
        == jnp.arange(extra, dtype=jnp.int32)[None, :]
    ).astype(jnp.bfloat16)
    payload = jnp.concatenate([tokens, seq_hot], axis=1)
    outgoing = lax.dot_general(
        placing, payload, (((0,), (0,)), ((), ())), preferred_element_type=jnp.float32
    )
    outgoing = jnp.concatenate(
        [outgoing[:, :model_width],
         lax.dot_general(combine, seq_hot, (((0,), (0,)), ((), ())),
                         preferred_element_type=jnp.float32)],
        axis=1,
    ).astype(jnp.bfloat16)
    outgoing = outgoing.reshape(experts, capacity, model_width + extra)
    arrived = lax.all_to_all(outgoing, "expert", split_axis=0, concat_axis=0, tiled=True)
    input_flat = arrived[:, :, :model_width].reshape(expert_size * capacity, model_width)
    my_meta = arrived[:, :, model_width:model_width + seq_count].astype(jnp.float32)
    same_src = jnp.eye(expert_size, dtype=jnp.float32)
    meta_t = jnp.transpose(my_meta, (2, 0, 1))
    sel_gate = same_src[:, None, :, None] * meta_t[None, :, :, :]
    sel_gate = sel_gate.reshape(row_seqs, expert_size * capacity)

    pre_act = jnp.dot(input_flat, weight_in[0], preferred_element_type=jnp.float32)
    gelu_val, slope_flat = gelu_parts(pre_act)
    hidden = gelu_val.astype(jnp.bfloat16)
    seq_hidden = jnp.dot(sel_gate.astype(jnp.bfloat16), hidden, preferred_element_type=jnp.float32)
    moe_seq = split_dot(seq_hidden, weight_out[0], (((1,), (0,)), ((), ())))
    moe_back = lax.all_to_all(
        moe_seq.reshape(expert_size, seq_count, model_width), "expert",
        split_axis=0, concat_axis=0, tiled=True,
    )
    moe_mine = jnp.sum(moe_back, axis=0)

    token_sum = jnp.sum(tokens.astype(jnp.float32).reshape(seq_count, LEN, model_width), axis=1)
    pooled = (token_sum + moe_mine) / LEN
    row_scale = lax.rsqrt(jnp.sum(pooled * pooled, axis=1) + EPSILON)
    unit_vec = pooled * row_scale[:, None]
    query_vec = unit_vec.astype(jnp.bfloat16)
    prem_count = premises.shape[0]
    key_rows = lax.all_gather(premises, "dp", axis=0, tiled=True)
    key_scale = lax.rsqrt(jnp.sum(jnp.square(key_rows.astype(jnp.float32)), axis=1) + EPSILON)
    key_index = jnp.arange(key_rows.shape[0], dtype=jnp.int32)
    own_positive = lax.dynamic_slice_in_dim(positive, device * seq_count, seq_count)
    mask_row = lax.dynamic_index_in_dim(tile_mask, device, 0, keepdims=False)
    key_open = jnp.repeat(mask_row, prem_count) == 1
    weighted_sum, partition, pos_vec = contrast_terms(
        query_vec,
        key_rows,
        key_scale,
        key_open[None, :],
        key_index[None, :] == own_positive[:, None],
    )
    delta_unit = LOSS_SCALE * SCORE_SCALE * (weighted_sum / partition[:, None] - pos_vec)
    delta_pooled = row_scale[:, None] * (
        delta_unit - unit_vec * jnp.sum(unit_vec * delta_unit, axis=1, keepdims=True)
    )
    delta_seq = (delta_pooled / LEN).astype(jnp.bfloat16)
    delta_all = lax.all_gather(delta_seq, ("dp", "expert"), axis=0, tiled=True)
    delta_row = lax.dynamic_slice_in_dim(delta_all, dp_index * row_seqs, row_seqs)

    grad_flat = lax.dot_general(
        sel_gate.astype(jnp.bfloat16), delta_row, (((0,), (0,)), ((), ())),
        preferred_element_type=jnp.float32,
    ).astype(jnp.bfloat16)
    dhidden = lax.dot_general(
        grad_flat, weight_out[0], (((1,), (1,)), ((), ())), preferred_element_type=jnp.float32
    )
    delta_pre = (dhidden * slope_flat).astype(jnp.bfloat16)
    grad_in_term = lax.dot_general(
        input_flat, delta_pre, (((0,), (0,)), ((), ())), preferred_element_type=jnp.float32
    ).astype(jnp.bfloat16)
    grad_in = reduce_scatter_2d(grad_in_term, nx, ny, lax.rem(dp_index, nx), dp_index // nx)

    block = ffn_width // dp_size
    hidden_blocks = jnp.transpose(
        seq_hidden.reshape(row_seqs, dp_size, block), (1, 0, 2)
    )
    hidden_cols = lax.all_to_all(hidden_blocks, "dp", split_axis=0, concat_axis=0, tiled=True)
    hidden_cols = hidden_cols.reshape(dp_size * row_seqs, block)
    grad_out = split_dot(hidden_cols, delta_all, (((0,), (0,)), ((), ())))
    return (grad_in[None], grad_out[None])


def solution(mesh):
    in_specs = (
        P(("dp", "expert"), None),
        P(("dp", "expert"), None),
        P(),
        P("expert", None, None),
        P("expert", None, None),
        P("dp", None),
        P(),
        P(),
    )
    out_specs = (P("expert", "dp", None), P("expert", "dp", None))
    return jax.shard_map(
        on_device, mesh=mesh, in_specs=in_specs, out_specs=out_specs, check_vma=False
    )
```

```python
import jax
import jax.numpy as jnp
from jax import lax
from jax.sharding import PartitionSpec as P

LEN = 64


SCORE_SCALE = 20.0
LOSS_SCALE = 64.0
EPSILON = 1e-06
HIGHEST = lax.Precision.HIGHEST


def gelu_parts(pre_act):
    inner_arg = 0.7978845608028654 * (pre_act + 0.044715 * pre_act * pre_act * pre_act)
    tangent = jnp.tanh(inner_arg)
    gelu_val = 0.5 * pre_act * (1.0 + tangent)
    slope_val = 0.5 * (1.0 + tangent) + 0.5 * pre_act * (
        1.0 - tangent * tangent
    ) * 0.7978845608028654 * (1.0 + 0.134145 * pre_act * pre_act)
    return (gelu_val, slope_val)


def route_slots(expert_ids, logits, experts, capacity):
    pick_hot = expert_ids[:, :, None] == jnp.arange(experts, dtype=jnp.int32)[None, None, :]
    picked = jnp.sum(jnp.where(pick_hot, logits[:, None, :], jnp.zeros((), logits.dtype)), axis=2)
    gate_wts = jax.nn.sigmoid(picked - picked[:, ::-1]).astype(jnp.bfloat16)
    flat_ids = expert_ids.reshape(-1)
    flat_hot = (flat_ids[:, None] == jnp.arange(experts, dtype=jnp.int32)[None, :]).astype(
        jnp.int32
    )
    running = jnp.cumsum(flat_hot, axis=0)
    position = jnp.sum(running * flat_hot, axis=1) - 1
    slot_ids = flat_ids * capacity + position
    return (gate_wts, slot_ids.reshape(expert_ids.shape))


def split_dot(a, b, dims):
    a_hi = a.astype(jnp.bfloat16)
    a_lo = (a - a_hi.astype(jnp.float32)).astype(jnp.bfloat16)
    hi = lax.dot_general(a_hi, b, dims, preferred_element_type=jnp.float32)
    lo = lax.dot_general(a_lo, b, dims, preferred_element_type=jnp.float32)
    return hi + lo


def contrast_terms(query_vec, key_rows, key_scale, open_mask, pos_hot):
    include = jnp.logical_or(open_mask, pos_hot)
    scores = (
        SCORE_SCALE
        * lax.dot_general(
            query_vec, key_rows, (((1,), (1,)), ((), ())), preferred_element_type=jnp.float32
        )
        * key_scale[None, :]
    )
    exp_scores = jnp.where(include, jnp.exp(scores), jnp.zeros((), scores.dtype))
    partition = jnp.sum(exp_scores, axis=1)
    soft_weight = (exp_scores * key_scale[None, :]).astype(jnp.bfloat16)
    weighted_sum = jnp.dot(soft_weight, key_rows, preferred_element_type=jnp.float32)
    pos_scale = jnp.sum(
        jnp.where(pos_hot, key_scale[None, :], jnp.zeros((), key_scale.dtype)), axis=1
    )
    pos_vec = (
        jnp.dot(pos_hot.astype(jnp.bfloat16), key_rows, preferred_element_type=jnp.float32)
        * pos_scale[:, None]
    )
    return (weighted_sum, partition, pos_vec)


def ring_pairs(nx, ny, along_x, step):
    pairs = []
    for y in range(ny):
        for x in range(nx):
            if along_x:
                pairs.append((y * nx + x, y * nx + (x + step) % nx))
            else:
                pairs.append((y * nx + x, ((y + step) % ny) * nx + x))
    return pairs


def take_chunk(chunks, index, count):
    return lax.dynamic_index_in_dim(chunks, lax.rem(index + 2 * count, count), 0, keepdims=False)


def ring_start(chunks, count, pos):
    half = chunks.shape[-1] // 2
    fwd, bwd = chunks[..., :half], chunks[..., half:]
    return dict(fwd=fwd, bwd=bwd, count=count, pos=pos,
                acc_f=take_chunk(fwd, pos - 1, count).astype(jnp.float32),
                acc_b=take_chunk(bwd, pos + 1, count).astype(jnp.float32))


def ring_step(state, k, fwd_pairs, bwd_pairs):
    count, pos = state["count"], state["pos"]
    got_f = lax.ppermute(state["acc_f"].astype(jnp.bfloat16), "dp", fwd_pairs)
    got_b = lax.ppermute(state["acc_b"].astype(jnp.bfloat16), "dp", bwd_pairs)
    state = dict(state)
    state["acc_f"] = got_f.astype(jnp.float32) + take_chunk(state["fwd"], pos - 2 - k, count).astype(jnp.float32)
    state["acc_b"] = got_b.astype(jnp.float32) + take_chunk(state["bwd"], pos + 2 + k, count).astype(jnp.float32)
    return state


def ring_result(state):
    return jnp.concatenate([state["acc_f"], state["acc_b"]], axis=-1)


def reduce_scatter_2d(partial, nx, ny, x_pos, y_pos):
    rows = partial.shape[0] // (nx * ny)
    width = partial.shape[1]
    half = width // 2
    grid = partial.reshape(ny, nx, rows, width)
    first = jnp.transpose(grid[..., :half], (1, 0, 2, 3))
    second = grid[..., half:]
    x_f, x_b = ring_pairs(nx, ny, True, 1), ring_pairs(nx, ny, True, -1)
    y_f, y_b = ring_pairs(nx, ny, False, 1), ring_pairs(nx, ny, False, -1)
    ra = ring_start(first, nx, x_pos)
    rb = ring_start(second, ny, y_pos)
    for k in range(max(nx, ny) - 1):
        if k < nx - 1:
            ra = ring_step(ra, k, x_f, x_b)
        if k < ny - 1:
            rb = ring_step(rb, k, y_f, y_b)
    ra = ring_start(ring_result(ra), ny, y_pos)
    rb = ring_start(ring_result(rb), nx, x_pos)
    for k in range(max(nx, ny) - 1):
        if k < ny - 1:
            ra = ring_step(ra, k, y_f, y_b)
        if k < nx - 1:
            rb = ring_step(rb, k, x_f, x_b)
    return jnp.concatenate([ring_result(ra), ring_result(rb)], axis=-1)


def on_device(tokens, expert_ids, router, weight_in, weight_out, premises, positive, tile_mask):
    token_count, model_width = tokens.shape
    ffn_width = weight_in.shape[2]
    experts = router.shape[1]
    expert_size = lax.axis_size("expert")
    dp_size = lax.axis_size("dp")
    nx = 4
    ny = dp_size // nx
    capacity = 4 * token_count // expert_size
    slot_total = experts * capacity
    seq_count = token_count // LEN
    row_seqs = expert_size * seq_count
    dp_index = lax.axis_index("dp")
    col_index = lax.axis_index("expert")
    device = dp_index * expert_size + col_index

    logits = jnp.dot(tokens, router, preferred_element_type=jnp.float32)
    gate_wts, slot_ids = route_slots(expert_ids, logits, experts, capacity)
    slot_hot = slot_ids[:, :, None] == jnp.arange(slot_total, dtype=jnp.int32)[None, None, :]
    placing = jnp.sum(slot_hot.astype(jnp.bfloat16), axis=1)
    combine = jnp.sum(
        jnp.where(slot_hot, gate_wts[:, :, None], jnp.zeros((), jnp.bfloat16)), axis=1
    )
    extra = 128
    seq_hot = (
        (jnp.arange(token_count, dtype=jnp.int32) // LEN)[:, None]
        == jnp.arange(extra, dtype=jnp.int32)[None, :]
    ).astype(jnp.bfloat16)
    payload = jnp.concatenate([tokens, seq_hot], axis=1)
    outgoing = lax.dot_general(
        placing, payload, (((0,), (0,)), ((), ())), preferred_element_type=jnp.float32
    )
    outgoing = jnp.concatenate(
        [outgoing[:, :model_width],
         lax.dot_general(combine, seq_hot, (((0,), (0,)), ((), ())),
                         preferred_element_type=jnp.float32)],
        axis=1,
    ).astype(jnp.bfloat16)
    outgoing = outgoing.reshape(experts, capacity, model_width + extra)
    arrived = lax.all_to_all(outgoing, "expert", split_axis=0, concat_axis=0, tiled=True)
    input_flat = arrived[:, :, :model_width].reshape(expert_size * capacity, model_width)
    my_meta = arrived[:, :, model_width:model_width + seq_count].astype(jnp.float32)
    same_src = jnp.eye(expert_size, dtype=jnp.float32)
    meta_t = jnp.transpose(my_meta, (2, 0, 1))
    sel_gate = same_src[:, None, :, None] * meta_t[None, :, :, :]
    sel_gate = sel_gate.reshape(row_seqs, expert_size * capacity)

    pre_act = jnp.dot(input_flat, weight_in[0], preferred_element_type=jnp.float32)
    gelu_val, slope_flat = gelu_parts(pre_act)
    hidden = gelu_val.astype(jnp.bfloat16)
    seq_hidden = jnp.dot(sel_gate.astype(jnp.bfloat16), hidden, preferred_element_type=jnp.float32)
    moe_seq = split_dot(seq_hidden, weight_out[0], (((1,), (0,)), ((), ())))
    moe_back = lax.all_to_all(
        moe_seq.reshape(expert_size, seq_count, model_width), "expert",
        split_axis=0, concat_axis=0, tiled=True,
    )
    moe_mine = jnp.sum(moe_back, axis=0)

    token_sum = jnp.sum(tokens.astype(jnp.float32).reshape(seq_count, LEN, model_width), axis=1)
    pooled = (token_sum + moe_mine) / LEN
    row_scale = lax.rsqrt(jnp.sum(pooled * pooled, axis=1) + EPSILON)
    unit_vec = pooled * row_scale[:, None]
    query_vec = unit_vec.astype(jnp.bfloat16)
    prem_count = premises.shape[0]
    key_rows = lax.all_gather(premises, "dp", axis=0, tiled=True)
    key_scale = lax.rsqrt(jnp.sum(jnp.square(key_rows.astype(jnp.float32)), axis=1) + EPSILON)
    key_index = jnp.arange(key_rows.shape[0], dtype=jnp.int32)
    own_positive = lax.dynamic_slice_in_dim(positive, device * seq_count, seq_count)
    mask_row = lax.dynamic_index_in_dim(tile_mask, device, 0, keepdims=False)
    key_open = jnp.repeat(mask_row, prem_count) == 1
    weighted_sum, partition, pos_vec = contrast_terms(
        query_vec,
        key_rows,
        key_scale,
        key_open[None, :],
        key_index[None, :] == own_positive[:, None],
    )
    delta_unit = LOSS_SCALE * SCORE_SCALE * (weighted_sum / partition[:, None] - pos_vec)
    delta_pooled = row_scale[:, None] * (
        delta_unit - unit_vec * jnp.sum(unit_vec * delta_unit, axis=1, keepdims=True)
    )
    delta_seq = (delta_pooled / LEN).astype(jnp.bfloat16)
    delta_row = lax.all_gather(delta_seq, "expert", axis=0, tiled=True)

    dims_t = (((0,), (0,)), ((), ()))
    spread = lax.dot_general(
        delta_row, weight_out[0], (((1,), (1,)), ((), ())), preferred_element_type=jnp.float32
    )
    dhidden = split_dot(spread, sel_gate.astype(jnp.bfloat16), dims_t).T
    delta_pre = (dhidden * slope_flat).astype(jnp.bfloat16)
    grad_in_term = lax.dot_general(
        input_flat, delta_pre, dims_t, preferred_element_type=jnp.float32
    ).astype(jnp.bfloat16)
    grad_out_term = split_dot(seq_hidden, delta_row, dims_t).astype(jnp.bfloat16)
    in_rows = model_width // dp_size
    out_rows = ffn_width // dp_size
    packed = jnp.concatenate(
        [grad_in_term.reshape(dp_size, in_rows, ffn_width),
         grad_out_term.reshape(dp_size, out_rows * model_width // ffn_width, ffn_width)],
        axis=1,
    )
    packed = packed.reshape(-1, ffn_width)
    total = reduce_scatter_2d(packed, nx, ny, lax.rem(dp_index, nx), dp_index // nx)
    grad_in = total[:in_rows]
    grad_out = total[in_rows:].reshape(out_rows, model_width)
    return (grad_in[None], grad_out[None])


def solution(mesh):
    in_specs = (
        P(("dp", "expert"), None),
        P(("dp", "expert"), None),
        P(),
        P("expert", None, None),
        P("expert", None, None),
        P("dp", None),
        P(),
        P(),
    )
    out_specs = (P("expert", "dp", None), P("expert", "dp", None))
    return jax.shard_map(
        on_device, mesh=mesh, in_specs=in_specs, out_specs=out_specs, check_vma=False
    )
```

```python
import jax
import jax.numpy as jnp
from jax import lax
from jax.sharding import PartitionSpec as P

LEN = 64


SCORE_SCALE = 20.0
LOSS_SCALE = 64.0
EPSILON = 1e-06
HIGHEST = lax.Precision.HIGHEST


def gelu_parts(pre_act):
    inner_arg = 0.7978845608028654 * (pre_act + 0.044715 * pre_act * pre_act * pre_act)
    tangent = jnp.tanh(inner_arg)
    gelu_val = 0.5 * pre_act * (1.0 + tangent)
    slope_val = 0.5 * (1.0 + tangent) + 0.5 * pre_act * (
        1.0 - tangent * tangent
    ) * 0.7978845608028654 * (1.0 + 0.134145 * pre_act * pre_act)
    return (gelu_val, slope_val)


def route_slots(expert_ids, logits, experts, capacity):
    pick_hot = expert_ids[:, :, None] == jnp.arange(experts, dtype=jnp.int32)[None, None, :]
    picked = jnp.sum(jnp.where(pick_hot, logits[:, None, :], jnp.zeros((), logits.dtype)), axis=2)
    gate_wts = jax.nn.sigmoid(picked - picked[:, ::-1]).astype(jnp.bfloat16)
    flat_ids = expert_ids.reshape(-1)
    flat_hot = (flat_ids[:, None] == jnp.arange(experts, dtype=jnp.int32)[None, :]).astype(
        jnp.int32
    )
    running = jnp.cumsum(flat_hot, axis=0)
    position = jnp.sum(running * flat_hot, axis=1) - 1
    slot_ids = flat_ids * capacity + position
    return (gate_wts, slot_ids.reshape(expert_ids.shape))


def split_dot(a, b, dims):
    a_hi = a.astype(jnp.bfloat16)
    a_lo = (a - a_hi.astype(jnp.float32)).astype(jnp.bfloat16)
    hi = lax.dot_general(a_hi, b, dims, preferred_element_type=jnp.float32)
    lo = lax.dot_general(a_lo, b, dims, preferred_element_type=jnp.float32)
    return hi + lo


def contrast_terms(query_vec, key_rows, key_scale, open_mask, pos_hot):
    include = jnp.logical_or(open_mask, pos_hot)
    scores = (
        SCORE_SCALE
        * lax.dot_general(
            query_vec, key_rows, (((1,), (1,)), ((), ())), preferred_element_type=jnp.float32
        )
        * key_scale[None, :]
    )
    exp_scores = jnp.where(include, jnp.exp(scores), jnp.zeros((), scores.dtype))
    partition = jnp.sum(exp_scores, axis=1)
    soft_weight = (exp_scores * key_scale[None, :]).astype(jnp.bfloat16)
    weighted_sum = jnp.dot(soft_weight, key_rows, preferred_element_type=jnp.float32)
    pos_scale = jnp.sum(
        jnp.where(pos_hot, key_scale[None, :], jnp.zeros((), key_scale.dtype)), axis=1
    )
    pos_vec = (
        jnp.dot(pos_hot.astype(jnp.bfloat16), key_rows, preferred_element_type=jnp.float32)
        * pos_scale[:, None]
    )
    return (weighted_sum, partition, pos_vec)


def ring_pairs(nx, ny, along_x, step):
    pairs = []
    for y in range(ny):
        for x in range(nx):
            if along_x:
                pairs.append((y * nx + x, y * nx + (x + step) % nx))
            else:
                pairs.append((y * nx + x, ((y + step) % ny) * nx + x))
    return pairs


def take_chunk(chunks, index, count):
    return lax.dynamic_index_in_dim(chunks, lax.rem(index + 2 * count, count), 0, keepdims=False)


def ring_start(fwd, bwd, count, pos):
    return dict(fwd=fwd, bwd=bwd, count=count, pos=pos,
                acc_f=take_chunk(fwd, pos - 1, count).astype(jnp.float32),
                acc_b=take_chunk(bwd, pos + 1, count).astype(jnp.float32))


def ring_step(state, k, fwd_pairs, bwd_pairs):
    count, pos = state["count"], state["pos"]
    got_f = lax.ppermute(state["acc_f"].astype(jnp.bfloat16), "dp", fwd_pairs)
    got_b = lax.ppermute(state["acc_b"].astype(jnp.bfloat16), "dp", bwd_pairs)
    state = dict(state)
    state["acc_f"] = got_f.astype(jnp.float32) + take_chunk(state["fwd"], pos - 2 - k, count).astype(jnp.float32)
    state["acc_b"] = got_b.astype(jnp.float32) + take_chunk(state["bwd"], pos + 2 + k, count).astype(jnp.float32)
    return state


def reduce_scatter_2d(part_in, part_out, nx, ny, x_pos, y_pos):
    def grid(part):
        rows = part.shape[0] // (nx * ny)
        return part.reshape(ny, nx, rows, part.shape[1])

    gin, gout = grid(part_in), grid(part_out)
    hin, hout = gin.shape[-1] // 2, gout.shape[-1] // 2
    x_f, x_b = ring_pairs(nx, ny, True, 1), ring_pairs(nx, ny, True, -1)
    y_f, y_b = ring_pairs(nx, ny, False, 1), ring_pairs(nx, ny, False, -1)
    ra = ring_start(jnp.transpose(gin[..., :hin], (1, 0, 2, 3)),
                    jnp.transpose(gout[..., :hout], (1, 0, 2, 3)), nx, x_pos)
    rb = ring_start(gin[..., hin:], gout[..., hout:], ny, y_pos)
    for k in range(max(nx, ny) - 1):
        if k < nx - 1:
            ra = ring_step(ra, k, x_f, x_b)
        if k < ny - 1:
            rb = ring_step(rb, k, y_f, y_b)
    ra = ring_start(ra["acc_f"], ra["acc_b"], ny, y_pos)
    rb = ring_start(rb["acc_f"], rb["acc_b"], nx, x_pos)
    for k in range(max(nx, ny) - 1):
        if k < ny - 1:
            ra = ring_step(ra, k, y_f, y_b)
        if k < nx - 1:
            rb = ring_step(rb, k, x_f, x_b)
    total_in = jnp.concatenate([ra["acc_f"], rb["acc_f"]], axis=-1)
    total_out = jnp.concatenate([ra["acc_b"], rb["acc_b"]], axis=-1)
    return total_in, total_out


def on_device(tokens, expert_ids, router, weight_in, weight_out, premises, positive, tile_mask):
    token_count, model_width = tokens.shape
    ffn_width = weight_in.shape[2]
    experts = router.shape[1]
    expert_size = lax.axis_size("expert")
    dp_size = lax.axis_size("dp")
    nx = 4
    ny = dp_size // nx
    capacity = 4 * token_count // expert_size
    slot_total = experts * capacity
    seq_count = token_count // LEN
    row_seqs = expert_size * seq_count
    dp_index = lax.axis_index("dp")
    col_index = lax.axis_index("expert")
    device = dp_index * expert_size + col_index

    logits = jnp.dot(tokens, router, preferred_element_type=jnp.float32)
    gate_wts, slot_ids = route_slots(expert_ids, logits, experts, capacity)
    slot_hot = slot_ids[:, :, None] == jnp.arange(slot_total, dtype=jnp.int32)[None, None, :]
    placing = jnp.sum(slot_hot.astype(jnp.bfloat16), axis=1)
    combine = jnp.sum(
        jnp.where(slot_hot, gate_wts[:, :, None], jnp.zeros((), jnp.bfloat16)), axis=1
    )
    extra = 128
    seq_hot = (
        (jnp.arange(token_count, dtype=jnp.int32) // LEN)[:, None]
        == jnp.arange(extra, dtype=jnp.int32)[None, :]
    ).astype(jnp.bfloat16)
    payload = jnp.concatenate([tokens, seq_hot], axis=1)
    outgoing = lax.dot_general(
        placing, payload, (((0,), (0,)), ((), ())), preferred_element_type=jnp.float32
    )
    outgoing = jnp.concatenate(
        [outgoing[:, :model_width],
         lax.dot_general(combine, seq_hot, (((0,), (0,)), ((), ())),
                         preferred_element_type=jnp.float32)],
        axis=1,
    ).astype(jnp.bfloat16)
    outgoing = outgoing.reshape(experts, capacity, model_width + extra)
    arrived = lax.all_to_all(outgoing, "expert", split_axis=0, concat_axis=0, tiled=True)
    input_flat = arrived[:, :, :model_width].reshape(expert_size * capacity, model_width)
    my_meta = arrived[:, :, model_width:model_width + seq_count].astype(jnp.float32)
    same_src = jnp.eye(expert_size, dtype=jnp.float32)
    meta_t = jnp.transpose(my_meta, (2, 0, 1))
    sel_gate = same_src[:, None, :, None] * meta_t[None, :, :, :]
    sel_gate = sel_gate.reshape(row_seqs, expert_size * capacity)

    pre_act = jnp.dot(input_flat, weight_in[0], preferred_element_type=jnp.float32)
    gelu_val, slope_flat = gelu_parts(pre_act)
    hidden = gelu_val.astype(jnp.bfloat16)
    seq_hidden = jnp.dot(sel_gate.astype(jnp.bfloat16), hidden, preferred_element_type=jnp.float32)
    moe_seq = split_dot(seq_hidden, weight_out[0], (((1,), (0,)), ((), ())))
    moe_back = lax.all_to_all(
        moe_seq.reshape(expert_size, seq_count, model_width), "expert",
        split_axis=0, concat_axis=0, tiled=True,
    )
    moe_mine = jnp.sum(moe_back, axis=0)

    token_sum = jnp.sum(tokens.astype(jnp.float32).reshape(seq_count, LEN, model_width), axis=1)
    pooled = (token_sum + moe_mine) / LEN
    row_scale = lax.rsqrt(jnp.sum(pooled * pooled, axis=1) + EPSILON)
    unit_vec = pooled * row_scale[:, None]
    query_vec = unit_vec.astype(jnp.bfloat16)
    prem_count = premises.shape[0]
    key_rows = lax.all_gather(premises, "dp", axis=0, tiled=True)
    key_scale = lax.rsqrt(jnp.sum(jnp.square(key_rows.astype(jnp.float32)), axis=1) + EPSILON)
    key_index = jnp.arange(key_rows.shape[0], dtype=jnp.int32)
    own_positive = lax.dynamic_slice_in_dim(positive, device * seq_count, seq_count)
    mask_row = lax.dynamic_index_in_dim(tile_mask, device, 0, keepdims=False)
    key_open = jnp.repeat(mask_row, prem_count) == 1
    weighted_sum, partition, pos_vec = contrast_terms(
        query_vec,
        key_rows,
        key_scale,
        key_open[None, :],
        key_index[None, :] == own_positive[:, None],
    )
    delta_unit = LOSS_SCALE * SCORE_SCALE * (weighted_sum / partition[:, None] - pos_vec)
    delta_pooled = row_scale[:, None] * (
        delta_unit - unit_vec * jnp.sum(unit_vec * delta_unit, axis=1, keepdims=True)
    )
    delta_seq = (delta_pooled / LEN).astype(jnp.bfloat16)
    delta_row = lax.all_gather(delta_seq, "expert", axis=0, tiled=True)

    dims_t = (((0,), (0,)), ((), ()))
    spread = lax.dot_general(
        delta_row, weight_out[0], (((1,), (1,)), ((), ())), preferred_element_type=jnp.float32
    ).astype(jnp.bfloat16)
    dhidden = lax.dot_general(
        sel_gate.astype(jnp.bfloat16), spread, dims_t, preferred_element_type=jnp.float32
    )
    delta_pre = (dhidden * slope_flat).astype(jnp.bfloat16)
    grad_in_term = lax.dot_general(
        input_flat, delta_pre, dims_t, preferred_element_type=jnp.float32
    ).astype(jnp.bfloat16)
    grad_out_term = lax.dot_general(
        seq_hidden.astype(jnp.bfloat16), delta_row, dims_t, preferred_element_type=jnp.float32
    ).astype(jnp.bfloat16)
    grad_in, grad_out = reduce_scatter_2d(
        grad_in_term, grad_out_term, nx, ny, lax.rem(dp_index, nx), dp_index // nx
    )
    return (grad_in[None], grad_out[None])


def solution(mesh):
    in_specs = (
        P(("dp", "expert"), None),
        P(("dp", "expert"), None),
        P(),
        P("expert", None, None),
        P("expert", None, None),
        P("dp", None),
        P(),
        P(),
    )
    out_specs = (P("expert", "dp", None), P("expert", "dp", None))
    return jax.shard_map(
        on_device, mesh=mesh, in_specs=in_specs, out_specs=out_specs, check_vma=False
    )
```

```python
import jax
import jax.numpy as jnp
from jax import lax
from jax.sharding import PartitionSpec as P

LEN = 64


SCORE_SCALE = 20.0
LOSS_SCALE = 64.0
EPSILON = 1e-06
HIGHEST = lax.Precision.HIGHEST


def gelu_parts(pre_act):
    inner_arg = 0.7978845608028654 * (pre_act + 0.044715 * pre_act * pre_act * pre_act)
    tangent = jnp.tanh(inner_arg)
    gelu_val = 0.5 * pre_act * (1.0 + tangent)
    slope_val = 0.5 * (1.0 + tangent) + 0.5 * pre_act * (
        1.0 - tangent * tangent
    ) * 0.7978845608028654 * (1.0 + 0.134145 * pre_act * pre_act)
    return (gelu_val, slope_val)


def route_slots(expert_ids, logits, experts, capacity):
    pick_hot = expert_ids[:, :, None] == jnp.arange(experts, dtype=jnp.int32)[None, None, :]
    picked = jnp.sum(jnp.where(pick_hot, logits[:, None, :], jnp.zeros((), logits.dtype)), axis=2)
    gate_wts = jax.nn.sigmoid(picked - picked[:, ::-1]).astype(jnp.bfloat16)
    flat_ids = expert_ids.reshape(-1)
    flat_hot = (flat_ids[:, None] == jnp.arange(experts, dtype=jnp.int32)[None, :]).astype(
        jnp.int32
    )
    running = jnp.cumsum(flat_hot, axis=0)
    position = jnp.sum(running * flat_hot, axis=1) - 1
    slot_ids = flat_ids * capacity + position
    return (gate_wts, slot_ids.reshape(expert_ids.shape))


def split_dot(a, b, dims):
    a_hi = a.astype(jnp.bfloat16)
    a_lo = (a - a_hi.astype(jnp.float32)).astype(jnp.bfloat16)
    hi = lax.dot_general(a_hi, b, dims, preferred_element_type=jnp.float32)
    lo = lax.dot_general(a_lo, b, dims, preferred_element_type=jnp.float32)
    return hi + lo


def contrast_terms(query_vec, key_rows, key_scale, open_mask, pos_hot):
    include = jnp.logical_or(open_mask, pos_hot)
    scores = (
        SCORE_SCALE
        * lax.dot_general(
            query_vec, key_rows, (((1,), (1,)), ((), ())), preferred_element_type=jnp.float32
        )
        * key_scale[None, :]
    )
    exp_scores = jnp.where(include, jnp.exp(scores), jnp.zeros((), scores.dtype))
    partition = jnp.sum(exp_scores, axis=1)
    soft_weight = (exp_scores * key_scale[None, :]).astype(jnp.bfloat16)
    weighted_sum = jnp.dot(soft_weight, key_rows, preferred_element_type=jnp.float32)
    pos_scale = jnp.sum(
        jnp.where(pos_hot, key_scale[None, :], jnp.zeros((), key_scale.dtype)), axis=1
    )
    pos_vec = (
        jnp.dot(pos_hot.astype(jnp.bfloat16), key_rows, preferred_element_type=jnp.float32)
        * pos_scale[:, None]
    )
    return (weighted_sum, partition, pos_vec)


def ring_pairs(nx, ny, along_x, step):
    pairs = []
    for y in range(ny):
        for x in range(nx):
            if along_x:
                pairs.append((y * nx + x, y * nx + (x + step) % nx))
            else:
                pairs.append((y * nx + x, ((y + step) % ny) * nx + x))
    return pairs


def take_chunk(chunks, index, count, axis=0):
    return lax.dynamic_index_in_dim(chunks, lax.rem(index + 4 * count, count), axis, keepdims=False)


def run_rings(rings):
    accs = []
    for streams, count, pos, _, _ in rings:
        accs.append([take_chunk(c, pos - d, count, ax).astype(jnp.float32) for c, ax, d in streams])
    for k in range(max(r[1] for r in rings) - 1):
        for i, (streams, count, pos, fwd_pairs, bwd_pairs) in enumerate(rings):
            if k >= count - 1:
                continue
            new = []
            for (c, ax, d), acc in zip(streams, accs[i]):
                got = lax.ppermute(acc.astype(jnp.bfloat16), "dp", fwd_pairs if d > 0 else bwd_pairs)
                new.append(got.astype(jnp.float32) + take_chunk(c, pos - d * (2 + k), count, ax).astype(jnp.float32))
            accs[i] = new
    return accs


def factored_sum(own, count, pos, along_x, nx, ny, width):
    parts = [own(pos)]
    for shift in range(1, count):
        parts.append(lax.ppermute(own(pos + shift), "dp", ring_pairs(nx, ny, along_x, shift)))
    stacked = jnp.concatenate(parts, axis=0)
    return lax.dot_general(
        stacked[:, :-width], stacked[:, -width:], (((0,), (0,)), ((), ())),
        preferred_element_type=jnp.float32,
    )


def reduce_scatter_2d(part_in, hidden_sum, delta_rows, nx, ny, x_pos, y_pos):
    rows = part_in.shape[0] // (nx * ny)
    width = part_in.shape[1]
    gin = part_in.reshape(ny, nx, rows, width)
    q = width // 4
    seqs, ffn = hidden_sum.shape
    out_rows = ffn // (nx * ny)
    model = delta_rows.shape[1]
    half_m = model // 2
    a4 = hidden_sum.astype(jnp.bfloat16).reshape(seqs, ny, nx, out_rows)
    x_f, x_b = ring_pairs(nx, ny, True, 1), ring_pairs(nx, ny, True, -1)
    y_f, y_b = ring_pairs(nx, ny, False, 1), ring_pairs(nx, ny, False, -1)

    def own_a(i):
        chunk = take_chunk(a4, i, nx, 2).reshape(seqs, ny * out_rows)
        return jnp.concatenate([chunk, delta_rows[:, :half_m]], axis=1)

    def own_b(i):
        chunk = take_chunk(a4, i, ny, 1).reshape(seqs, nx * out_rows)
        return jnp.concatenate([chunk, delta_rows[:, half_m:]], axis=1)

    out_a = factored_sum(own_a, nx, x_pos, True, nx, ny, half_m).reshape(ny, out_rows, half_m)
    out_b = factored_sum(own_b, ny, y_pos, False, nx, ny, half_m).reshape(nx, out_rows, half_m)
    first = run_rings([
        ([(gin[..., 0:q], 1, 1), (gin[..., q:2 * q], 1, -1)], nx, x_pos, x_f, x_b),
        ([(gin[..., 2 * q:3 * q], 0, 1), (gin[..., 3 * q:], 0, -1)], ny, y_pos, y_f, y_b),
    ])
    in_a = jnp.concatenate(first[0], axis=-1)
    in_b = jnp.concatenate(first[1], axis=-1)
    second = run_rings([
        ([(in_a, 0, 1), (out_a, 0, -1)], ny, y_pos, y_f, y_b),
        ([(in_b, 0, 1), (out_b, 0, -1)], nx, x_pos, x_f, x_b),
    ])
    total_in = jnp.concatenate([second[0][0], second[1][0]], axis=-1)
    total_out = jnp.concatenate([second[0][1], second[1][1]], axis=-1)
    return total_in, total_out


def on_device(tokens, expert_ids, router, weight_in, weight_out, premises, positive, tile_mask):
    token_count, model_width = tokens.shape
    ffn_width = weight_in.shape[2]
    experts = router.shape[1]
    expert_size = lax.axis_size("expert")
    dp_size = lax.axis_size("dp")
    nx = 4
    ny = dp_size // nx
    capacity = 4 * token_count // expert_size
    slot_total = experts * capacity
    seq_count = token_count // LEN
    row_seqs = expert_size * seq_count
    dp_index = lax.axis_index("dp")
    col_index = lax.axis_index("expert")
    device = dp_index * expert_size + col_index

    logits = jnp.dot(tokens, router, preferred_element_type=jnp.float32)
    gate_wts, slot_ids = route_slots(expert_ids, logits, experts, capacity)
    slot_hot = slot_ids[:, :, None] == jnp.arange(slot_total, dtype=jnp.int32)[None, None, :]
    placing = jnp.sum(slot_hot.astype(jnp.bfloat16), axis=1)
    combine = jnp.sum(
        jnp.where(slot_hot, gate_wts[:, :, None], jnp.zeros((), jnp.bfloat16)), axis=1
    )
    extra = 128
    seq_hot = (
        (jnp.arange(token_count, dtype=jnp.int32) // LEN)[:, None]
        == jnp.arange(extra, dtype=jnp.int32)[None, :]
    ).astype(jnp.bfloat16)
    payload = jnp.concatenate([tokens, seq_hot], axis=1)
    outgoing = lax.dot_general(
        placing, payload, (((0,), (0,)), ((), ())), preferred_element_type=jnp.float32
    )
    outgoing = jnp.concatenate(
        [outgoing[:, :model_width],
         lax.dot_general(combine, seq_hot, (((0,), (0,)), ((), ())),
                         preferred_element_type=jnp.float32)],
        axis=1,
    ).astype(jnp.bfloat16)
    outgoing = outgoing.reshape(experts, capacity, model_width + extra)
    arrived = lax.all_to_all(outgoing, "expert", split_axis=0, concat_axis=0, tiled=True)
    input_flat = arrived[:, :, :model_width].reshape(expert_size * capacity, model_width)
    my_meta = arrived[:, :, model_width:model_width + seq_count].astype(jnp.float32)
    same_src = jnp.eye(expert_size, dtype=jnp.float32)
    meta_t = jnp.transpose(my_meta, (2, 0, 1))
    sel_gate = same_src[:, None, :, None] * meta_t[None, :, :, :]
    sel_gate = sel_gate.reshape(row_seqs, expert_size * capacity)

    pre_act = jnp.dot(input_flat, weight_in[0], preferred_element_type=jnp.float32)
    gelu_val, slope_flat = gelu_parts(pre_act)
    hidden = gelu_val.astype(jnp.bfloat16)
    seq_hidden = jnp.dot(sel_gate.astype(jnp.bfloat16), hidden, preferred_element_type=jnp.float32)
    moe_seq = split_dot(seq_hidden, weight_out[0], (((1,), (0,)), ((), ())))
    moe_back = lax.all_to_all(
        moe_seq.reshape(expert_size, seq_count, model_width), "expert",
        split_axis=0, concat_axis=0, tiled=True,
    )
    moe_mine = jnp.sum(moe_back, axis=0)

    token_sum = jnp.sum(tokens.astype(jnp.float32).reshape(seq_count, LEN, model_width), axis=1)
    pooled = (token_sum + moe_mine) / LEN
    row_scale = lax.rsqrt(jnp.sum(pooled * pooled, axis=1) + EPSILON)
    unit_vec = pooled * row_scale[:, None]
    query_vec = unit_vec.astype(jnp.bfloat16)
    prem_count = premises.shape[0]
    key_rows = lax.all_gather(premises, "dp", axis=0, tiled=True)
    key_scale = lax.rsqrt(jnp.sum(jnp.square(key_rows.astype(jnp.float32)), axis=1) + EPSILON)
    key_index = jnp.arange(key_rows.shape[0], dtype=jnp.int32)
    own_positive = lax.dynamic_slice_in_dim(positive, device * seq_count, seq_count)
    mask_row = lax.dynamic_index_in_dim(tile_mask, device, 0, keepdims=False)
    key_open = jnp.repeat(mask_row, prem_count) == 1
    weighted_sum, partition, pos_vec = contrast_terms(
        query_vec,
        key_rows,
        key_scale,
        key_open[None, :],
        key_index[None, :] == own_positive[:, None],
    )
    delta_unit = LOSS_SCALE * SCORE_SCALE * (weighted_sum / partition[:, None] - pos_vec)
    delta_pooled = row_scale[:, None] * (
        delta_unit - unit_vec * jnp.sum(unit_vec * delta_unit, axis=1, keepdims=True)
    )
    delta_seq = (delta_pooled / LEN).astype(jnp.bfloat16)
    delta_row = lax.all_gather(delta_seq, "expert", axis=0, tiled=True)

    dims_t = (((0,), (0,)), ((), ()))
    spread = lax.dot_general(
        delta_row, weight_out[0], (((1,), (1,)), ((), ())), preferred_element_type=jnp.float32
    ).astype(jnp.bfloat16)
    dhidden = lax.dot_general(
        sel_gate.astype(jnp.bfloat16), spread, dims_t, preferred_element_type=jnp.float32
    )
    delta_pre = (dhidden * slope_flat).astype(jnp.bfloat16)
    grad_in_term = lax.dot_general(
        input_flat, delta_pre, dims_t, preferred_element_type=jnp.float32
    ).astype(jnp.bfloat16)
    grad_in, grad_out = reduce_scatter_2d(
        grad_in_term, seq_hidden, delta_row, nx, ny, lax.rem(dp_index, nx), dp_index // nx
    )
    return (grad_in[None], grad_out[None])


def solution(mesh):
    in_specs = (
        P(("dp", "expert"), None),
        P(("dp", "expert"), None),
        P(),
        P("expert", None, None),
        P("expert", None, None),
        P("dp", None),
        P(),
        P(),
    )
    out_specs = (P("expert", "dp", None), P("expert", "dp", None))
    return jax.shard_map(
        on_device, mesh=mesh, in_specs=in_specs, out_specs=out_specs, check_vma=False
    )
```

```python
import jax
import jax.numpy as jnp
from jax import lax
from jax.sharding import PartitionSpec as P

LEN = 64


SCORE_SCALE = 20.0
LOSS_SCALE = 64.0
EPSILON = 1e-06
HIGHEST = lax.Precision.HIGHEST


def gelu_parts(pre_act):
    inner_arg = 0.7978845608028654 * (pre_act + 0.044715 * pre_act * pre_act * pre_act)
    tangent = jnp.tanh(inner_arg)
    gelu_val = 0.5 * pre_act * (1.0 + tangent)
    slope_val = 0.5 * (1.0 + tangent) + 0.5 * pre_act * (
        1.0 - tangent * tangent
    ) * 0.7978845608028654 * (1.0 + 0.134145 * pre_act * pre_act)
    return (gelu_val, slope_val)


def route_slots(expert_ids, logits, experts, capacity):
    pick_hot = expert_ids[:, :, None] == jnp.arange(experts, dtype=jnp.int32)[None, None, :]
    picked = jnp.sum(jnp.where(pick_hot, logits[:, None, :], jnp.zeros((), logits.dtype)), axis=2)
    gate_wts = jax.nn.sigmoid(picked - picked[:, ::-1]).astype(jnp.bfloat16)
    flat_ids = expert_ids.reshape(-1)
    flat_hot = (flat_ids[:, None] == jnp.arange(experts, dtype=jnp.int32)[None, :]).astype(
        jnp.int32
    )
    running = jnp.cumsum(flat_hot, axis=0)
    position = jnp.sum(running * flat_hot, axis=1) - 1
    slot_ids = flat_ids * capacity + position
    return (gate_wts, slot_ids.reshape(expert_ids.shape))


def split_dot(a, b, dims):
    a_hi = a.astype(jnp.bfloat16)
    a_lo = (a - a_hi.astype(jnp.float32)).astype(jnp.bfloat16)
    hi = lax.dot_general(a_hi, b, dims, preferred_element_type=jnp.float32)
    lo = lax.dot_general(a_lo, b, dims, preferred_element_type=jnp.float32)
    return hi + lo


def contrast_terms(query_vec, key_rows, key_scale, open_mask, pos_hot):
    include = jnp.logical_or(open_mask, pos_hot)
    scores = (
        SCORE_SCALE
        * lax.dot_general(
            query_vec, key_rows, (((1,), (1,)), ((), ())), preferred_element_type=jnp.float32
        )
        * key_scale[None, :]
    )
    exp_scores = jnp.where(include, jnp.exp(scores), jnp.zeros((), scores.dtype))
    partition = jnp.sum(exp_scores, axis=1)
    soft_weight = (exp_scores * key_scale[None, :]).astype(jnp.bfloat16)
    weighted_sum = jnp.dot(soft_weight, key_rows, preferred_element_type=jnp.float32)
    pos_scale = jnp.sum(
        jnp.where(pos_hot, key_scale[None, :], jnp.zeros((), key_scale.dtype)), axis=1
    )
    pos_vec = (
        jnp.dot(pos_hot.astype(jnp.bfloat16), key_rows, preferred_element_type=jnp.float32)
        * pos_scale[:, None]
    )
    return (weighted_sum, partition, pos_vec)


def ring_pairs(nx, ny, along_x, step):
    pairs = []
    for y in range(ny):
        for x in range(nx):
            if along_x:
                pairs.append((y * nx + x, y * nx + (x + step) % nx))
            else:
                pairs.append((y * nx + x, ((y + step) % ny) * nx + x))
    return pairs


def take_chunk(chunks, index, count, axis=0):
    return lax.dynamic_index_in_dim(chunks, lax.rem(index + 2 * count, count), axis, keepdims=False)


def ring_start(fwd, bwd, count, pos, axis=0):
    return dict(fwd=fwd, bwd=bwd, count=count, pos=pos, axis=axis,
                acc_f=take_chunk(fwd, pos - 1, count, axis).astype(jnp.float32),
                acc_b=take_chunk(bwd, pos + 1, count, axis).astype(jnp.float32))


def ring_step(state, k, fwd_pairs, bwd_pairs):
    count, pos, axis = state["count"], state["pos"], state["axis"]
    got_f = lax.ppermute(state["acc_f"].astype(jnp.bfloat16), "dp", fwd_pairs)
    got_b = lax.ppermute(state["acc_b"].astype(jnp.bfloat16), "dp", bwd_pairs)
    state = dict(state)
    state["acc_f"] = got_f.astype(jnp.float32) + take_chunk(state["fwd"], pos - 2 - k, count, axis).astype(jnp.float32)
    state["acc_b"] = got_b.astype(jnp.float32) + take_chunk(state["bwd"], pos + 2 + k, count, axis).astype(jnp.float32)
    return state


def reduce_scatter_2d(part_in, part_out, nx, ny, x_pos, y_pos):
    def grid(part):
        rows = part.shape[0] // (nx * ny)
        return part.reshape(ny, nx, rows, part.shape[1])

    gin, gout = grid(part_in), grid(part_out)
    hin, hout = gin.shape[-1] // 2, gout.shape[-1] // 2
    x_f, x_b = ring_pairs(nx, ny, True, 1), ring_pairs(nx, ny, True, -1)
    y_f, y_b = ring_pairs(nx, ny, False, 1), ring_pairs(nx, ny, False, -1)
    ra = ring_start(gin[..., :hin], gout[..., :hout], nx, x_pos, axis=1)
    rb = ring_start(gin[..., hin:], gout[..., hout:], ny, y_pos)
    for k in range(max(nx, ny) - 1):
        if k < nx - 1:
            ra = ring_step(ra, k, x_f, x_b)
        if k < ny - 1:
            rb = ring_step(rb, k, y_f, y_b)
    ra = ring_start(ra["acc_f"], ra["acc_b"], ny, y_pos)
    rb = ring_start(rb["acc_f"], rb["acc_b"], nx, x_pos)
    for k in range(max(nx, ny) - 1):
        if k < ny - 1:
            ra = ring_step(ra, k, y_f, y_b)
        if k < nx - 1:
            rb = ring_step(rb, k, x_f, x_b)
    total_in = jnp.concatenate([ra["acc_f"], rb["acc_f"]], axis=-1)
    total_out = jnp.concatenate([ra["acc_b"], rb["acc_b"]], axis=-1)
    return total_in, total_out


def on_device(tokens, expert_ids, router, weight_in, weight_out, premises, positive, tile_mask):
    token_count, model_width = tokens.shape
    ffn_width = weight_in.shape[2]
    experts = router.shape[1]
    expert_size = lax.axis_size("expert")
    dp_size = lax.axis_size("dp")
    nx = 4
    ny = dp_size // nx
    capacity = 4 * token_count // expert_size
    slot_total = experts * capacity
    seq_count = token_count // LEN
    row_seqs = expert_size * seq_count
    dp_index = lax.axis_index("dp")
    col_index = lax.axis_index("expert")
    device = dp_index * expert_size + col_index

    logits = jnp.dot(tokens, router, preferred_element_type=jnp.float32)
    gate_wts, slot_ids = route_slots(expert_ids, logits, experts, capacity)
    slot_hot = slot_ids[:, :, None] == jnp.arange(slot_total, dtype=jnp.int32)[None, None, :]
    placing = jnp.sum(slot_hot.astype(jnp.bfloat16), axis=1)
    combine = jnp.sum(
        jnp.where(slot_hot, gate_wts[:, :, None], jnp.zeros((), jnp.bfloat16)), axis=1
    )
    extra = 128
    seq_hot = (
        (jnp.arange(token_count, dtype=jnp.int32) // LEN)[:, None]
        == jnp.arange(extra, dtype=jnp.int32)[None, :]
    ).astype(jnp.bfloat16)
    payload = jnp.concatenate([tokens, seq_hot], axis=1)
    outgoing = lax.dot_general(
        placing, payload, (((0,), (0,)), ((), ())), preferred_element_type=jnp.float32
    )
    outgoing = jnp.concatenate(
        [outgoing[:, :model_width],
         lax.dot_general(combine, seq_hot, (((0,), (0,)), ((), ())),
                         preferred_element_type=jnp.float32)],
        axis=1,
    ).astype(jnp.bfloat16)
    outgoing = outgoing.reshape(experts, capacity, model_width + extra)
    arrived = lax.all_to_all(outgoing, "expert", split_axis=0, concat_axis=0, tiled=True)
    input_flat = arrived[:, :, :model_width].reshape(expert_size * capacity, model_width)
    my_meta = arrived[:, :, model_width:model_width + seq_count].astype(jnp.float32)
    same_src = jnp.eye(expert_size, dtype=jnp.float32)
    meta_t = jnp.transpose(my_meta, (2, 0, 1))
    sel_gate = same_src[:, None, :, None] * meta_t[None, :, :, :]
    sel_gate = sel_gate.reshape(row_seqs, expert_size * capacity)

    pre_act = jnp.dot(input_flat, weight_in[0], preferred_element_type=jnp.float32)
    gelu_val, slope_flat = gelu_parts(pre_act)
    hidden = gelu_val.astype(jnp.bfloat16)
    seq_hidden = jnp.dot(sel_gate.astype(jnp.bfloat16), hidden, preferred_element_type=jnp.float32)
    moe_seq = split_dot(seq_hidden, weight_out[0], (((1,), (0,)), ((), ())))
    moe_back = lax.all_to_all(
        moe_seq.reshape(expert_size, seq_count, model_width), "expert",
        split_axis=0, concat_axis=0, tiled=True,
    )
    moe_mine = jnp.sum(moe_back, axis=0)

    token_sum = jnp.sum(tokens.astype(jnp.float32).reshape(seq_count, LEN, model_width), axis=1)
    pooled = (token_sum + moe_mine) / LEN
    row_scale = lax.rsqrt(jnp.sum(pooled * pooled, axis=1) + EPSILON)
    unit_vec = pooled * row_scale[:, None]
    query_vec = unit_vec.astype(jnp.bfloat16)
    prem_count = premises.shape[0]
    key_rows = lax.all_gather(premises, "dp", axis=0, tiled=True)
    key_scale = lax.rsqrt(jnp.sum(jnp.square(key_rows.astype(jnp.float32)), axis=1) + EPSILON)
    key_index = jnp.arange(key_rows.shape[0], dtype=jnp.int32)
    own_positive = lax.dynamic_slice_in_dim(positive, device * seq_count, seq_count)
    mask_row = lax.dynamic_index_in_dim(tile_mask, device, 0, keepdims=False)
    key_open = jnp.repeat(mask_row, prem_count) == 1
    weighted_sum, partition, pos_vec = contrast_terms(
        query_vec,
        key_rows,
        key_scale,
        key_open[None, :],
        key_index[None, :] == own_positive[:, None],
    )
    delta_unit = LOSS_SCALE * SCORE_SCALE * (weighted_sum / partition[:, None] - pos_vec)
    delta_pooled = row_scale[:, None] * (
        delta_unit - unit_vec * jnp.sum(unit_vec * delta_unit, axis=1, keepdims=True)
    )
    delta_seq = (delta_pooled / LEN).astype(jnp.bfloat16)
    delta_row = lax.all_gather(delta_seq, "expert", axis=0, tiled=True)

    dims_t = (((0,), (0,)), ((), ()))
    spread_t = lax.dot_general(
        weight_out[0], delta_row, (((1,), (1,)), ((), ())), preferred_element_type=jnp.float32
    ).astype(jnp.bfloat16)
    dhidden = lax.dot_general(
        sel_gate.astype(jnp.bfloat16), spread_t, (((0,), (1,)), ((), ())),
        preferred_element_type=jnp.float32,
    )
    delta_pre = lax.optimization_barrier((dhidden * slope_flat).astype(jnp.bfloat16))
    grad_in_term = lax.dot_general(
        input_flat, delta_pre, dims_t, preferred_element_type=jnp.float32
    ).astype(jnp.bfloat16)
    grad_out_term = lax.dot_general(
        seq_hidden.astype(jnp.bfloat16), delta_row, dims_t, preferred_element_type=jnp.float32
    ).astype(jnp.bfloat16)
    grad_in, grad_out = reduce_scatter_2d(
        grad_in_term, grad_out_term, nx, ny, lax.rem(dp_index, nx), dp_index // nx
    )
    return (grad_in[None], grad_out[None])


def solution(mesh):
    in_specs = (
        P(("dp", "expert"), None),
        P(("dp", "expert"), None),
        P(),
        P("expert", None, None),
        P("expert", None, None),
        P("dp", None),
        P(),
        P(),
    )
    out_specs = (P("expert", "dp", None), P("expert", "dp", None))
    return jax.shard_map(
        on_device, mesh=mesh, in_specs=in_specs, out_specs=out_specs, check_vma=False
    )
```

```python
import jax
import jax.numpy as jnp
from jax import lax
from jax.sharding import PartitionSpec as P

LEN = 64


SCORE_SCALE = 20.0
LOSS_SCALE = 64.0
EPSILON = 1e-06
HIGHEST = lax.Precision.HIGHEST


def gelu_parts(pre_act):
    inner_arg = 0.7978845608028654 * (pre_act + 0.044715 * pre_act * pre_act * pre_act)
    tangent = jnp.tanh(inner_arg)
    gelu_val = 0.5 * pre_act * (1.0 + tangent)
    slope_val = 0.5 * (1.0 + tangent) + 0.5 * pre_act * (
        1.0 - tangent * tangent
    ) * 0.7978845608028654 * (1.0 + 0.134145 * pre_act * pre_act)
    return (gelu_val, slope_val)


def route_slots(expert_ids, logits, experts, capacity):
    pick_hot = expert_ids[:, :, None] == jnp.arange(experts, dtype=jnp.int32)[None, None, :]
    picked = jnp.sum(jnp.where(pick_hot, logits[:, None, :], jnp.zeros((), logits.dtype)), axis=2)
    gate_wts = jax.nn.sigmoid(picked - picked[:, ::-1]).astype(jnp.bfloat16)
    flat_ids = expert_ids.reshape(-1)
    flat_hot = (flat_ids[:, None] == jnp.arange(experts, dtype=jnp.int32)[None, :]).astype(
        jnp.int32
    )
    running = jnp.cumsum(flat_hot, axis=0)
    position = jnp.sum(running * flat_hot, axis=1) - 1
    slot_ids = flat_ids * capacity + position
    return (gate_wts, slot_ids.reshape(expert_ids.shape))


def split_dot(a, b, dims):
    a_hi = a.astype(jnp.bfloat16)
    a_lo = (a - a_hi.astype(jnp.float32)).astype(jnp.bfloat16)
    hi = lax.dot_general(a_hi, b, dims, preferred_element_type=jnp.float32)
    lo = lax.dot_general(a_lo, b, dims, preferred_element_type=jnp.float32)
    return hi + lo


def contrast_terms(query_vec, key_rows, key_scale, open_mask, pos_hot):
    include = jnp.logical_or(open_mask, pos_hot)
    scores = (
        SCORE_SCALE
        * lax.dot_general(
            query_vec, key_rows, (((1,), (1,)), ((), ())), preferred_element_type=jnp.float32
        )
        * key_scale[None, :]
    )
    exp_scores = jnp.where(include, jnp.exp(scores), jnp.zeros((), scores.dtype))
    partition = jnp.sum(exp_scores, axis=1)
    soft_weight = (exp_scores * key_scale[None, :]).astype(jnp.bfloat16)
    weighted_sum = jnp.dot(soft_weight, key_rows, preferred_element_type=jnp.float32)
    pos_scale = jnp.sum(
        jnp.where(pos_hot, key_scale[None, :], jnp.zeros((), key_scale.dtype)), axis=1
    )
    pos_vec = (
        jnp.dot(pos_hot.astype(jnp.bfloat16), key_rows, preferred_element_type=jnp.float32)
        * pos_scale[:, None]
    )
    return (weighted_sum, partition, pos_vec)


def ring_pairs(nx, ny, along_x, step):
    pairs = []
    for y in range(ny):
        for x in range(nx):
            if along_x:
                pairs.append((y * nx + x, y * nx + (x + step) % nx))
            else:
                pairs.append((y * nx + x, ((y + step) % ny) * nx + x))
    return pairs


def take_chunk(chunks, index, count, axis=0):
    return lax.dynamic_index_in_dim(chunks, lax.rem(index + 2 * count, count), axis, keepdims=False)


def ring_start(fwd, bwd, count, pos, axis=0):
    return dict(fwd=fwd, bwd=bwd, count=count, pos=pos, axis=axis,
                acc_f=take_chunk(fwd, pos - 1, count, axis).astype(jnp.float32),
                acc_b=take_chunk(bwd, pos + 1, count, axis).astype(jnp.float32))


def ring_step(state, k, fwd_pairs, bwd_pairs):
    count, pos, axis = state["count"], state["pos"], state["axis"]
    got_f = lax.ppermute(state["acc_f"].astype(jnp.bfloat16), "dp", fwd_pairs)
    got_b = lax.ppermute(state["acc_b"].astype(jnp.bfloat16), "dp", bwd_pairs)
    state = dict(state)
    state["acc_f"] = got_f.astype(jnp.float32) + take_chunk(state["fwd"], pos - 2 - k, count, axis).astype(jnp.float32)
    state["acc_b"] = got_b.astype(jnp.float32) + take_chunk(state["bwd"], pos + 2 + k, count, axis).astype(jnp.float32)
    return state


def reduce_scatter_2d(part_in, part_out, nx, ny, x_pos, y_pos):
    def grid(part):
        rows = part.shape[0] // (nx * ny)
        return part.reshape(ny, nx, rows, part.shape[1])

    gin, gout = grid(part_in), grid(part_out)
    hin, hout = gin.shape[-1] // 2, gout.shape[-1] // 2
    x_f, x_b = ring_pairs(nx, ny, True, 1), ring_pairs(nx, ny, True, -1)
    y_f, y_b = ring_pairs(nx, ny, False, 1), ring_pairs(nx, ny, False, -1)
    ra = ring_start(gin[..., :hin], gout[..., :hout], nx, x_pos, axis=1)
    rb = ring_start(gin[..., hin:], gout[..., hout:], ny, y_pos)
    for k in range(max(nx, ny) - 1):
        if k < nx - 1:
            ra = ring_step(ra, k, x_f, x_b)
        if k < ny - 1:
            rb = ring_step(rb, k, y_f, y_b)
    ra = ring_start(ra["acc_f"], ra["acc_b"], ny, y_pos)
    rb = ring_start(rb["acc_f"], rb["acc_b"], nx, x_pos)
    for k in range(max(nx, ny) - 1):
        if k < ny - 1:
            ra = ring_step(ra, k, y_f, y_b)
        if k < nx - 1:
            rb = ring_step(rb, k, x_f, x_b)
    total_in = jnp.concatenate([ra["acc_f"], rb["acc_f"]], axis=-1)
    total_out = jnp.concatenate([ra["acc_b"], rb["acc_b"]], axis=-1)
    return total_in, total_out


def on_device(tokens, expert_ids, router, weight_in, weight_out, premises, positive, tile_mask):
    token_count, model_width = tokens.shape
    ffn_width = weight_in.shape[2]
    experts = router.shape[1]
    expert_size = lax.axis_size("expert")
    dp_size = lax.axis_size("dp")
    nx = 4
    ny = dp_size // nx
    capacity = 4 * token_count // expert_size
    slot_total = experts * capacity
    seq_count = token_count // LEN
    row_seqs = expert_size * seq_count
    dp_index = lax.axis_index("dp")
    col_index = lax.axis_index("expert")
    device = dp_index * expert_size + col_index

    logits = jnp.dot(tokens, router, preferred_element_type=jnp.float32)
    gate_wts, slot_ids = route_slots(expert_ids, logits, experts, capacity)
    slot_hot = slot_ids[:, :, None] == jnp.arange(slot_total, dtype=jnp.int32)[None, None, :]
    placing = jnp.sum(slot_hot.astype(jnp.bfloat16), axis=1)
    combine = jnp.sum(
        jnp.where(slot_hot, gate_wts[:, :, None], jnp.zeros((), jnp.bfloat16)), axis=1
    )
    extra = 128
    seq_hot = (
        (jnp.arange(token_count, dtype=jnp.int32) // LEN)[:, None]
        == jnp.arange(extra, dtype=jnp.int32)[None, :]
    ).astype(jnp.bfloat16)
    payload = jnp.concatenate([tokens, seq_hot], axis=1)
    outgoing = lax.dot_general(
        placing, payload, (((0,), (0,)), ((), ())), preferred_element_type=jnp.float32
    )
    outgoing = jnp.concatenate(
        [outgoing[:, :model_width],
         lax.dot_general(combine, seq_hot, (((0,), (0,)), ((), ())),
                         preferred_element_type=jnp.float32)],
        axis=1,
    ).astype(jnp.bfloat16)
    outgoing = outgoing.reshape(experts, capacity, model_width + extra)
    arrived = lax.all_to_all(outgoing, "expert", split_axis=0, concat_axis=0, tiled=True)
    input_flat = arrived[:, :, :model_width].reshape(expert_size * capacity, model_width)
    my_meta = arrived[:, :, model_width:model_width + seq_count].astype(jnp.float32)
    same_src = jnp.eye(expert_size, dtype=jnp.float32)
    meta_t = jnp.transpose(my_meta, (2, 0, 1))
    sel_gate = same_src[:, None, :, None] * meta_t[None, :, :, :]
    sel_gate = sel_gate.reshape(row_seqs, expert_size * capacity)

    pre_act = jnp.dot(input_flat, weight_in[0], preferred_element_type=jnp.float32)
    gelu_val, slope_flat = gelu_parts(pre_act)
    hidden = gelu_val.astype(jnp.bfloat16)
    seq_hidden = jnp.dot(sel_gate.astype(jnp.bfloat16), hidden, preferred_element_type=jnp.float32)
    moe_seq = split_dot(seq_hidden, weight_out[0], (((1,), (0,)), ((), ())))
    moe_back = lax.all_to_all(
        moe_seq.reshape(expert_size, seq_count, model_width), "expert",
        split_axis=0, concat_axis=0, tiled=True,
    )
    moe_mine = jnp.sum(moe_back, axis=0)

    token_sum = jnp.sum(tokens.astype(jnp.float32).reshape(seq_count, LEN, model_width), axis=1)
    pooled = (token_sum + moe_mine) / LEN
    row_scale = lax.rsqrt(jnp.sum(pooled * pooled, axis=1) + EPSILON)
    unit_vec = pooled * row_scale[:, None]
    query_vec = unit_vec.astype(jnp.bfloat16)
    prem_count = premises.shape[0]
    key_rows = lax.all_gather(premises, "dp", axis=0, tiled=True)
    key_scale = lax.rsqrt(jnp.sum(jnp.square(key_rows.astype(jnp.float32)), axis=1) + EPSILON)
    key_index = jnp.arange(key_rows.shape[0], dtype=jnp.int32)
    own_positive = lax.dynamic_slice_in_dim(positive, device * seq_count, seq_count)
    mask_row = lax.dynamic_index_in_dim(tile_mask, device, 0, keepdims=False)
    key_open = jnp.repeat(mask_row, prem_count) == 1
    weighted_sum, partition, pos_vec = contrast_terms(
        query_vec,
        key_rows,
        key_scale,
        key_open[None, :],
        key_index[None, :] == own_positive[:, None],
    )
    delta_unit = LOSS_SCALE * SCORE_SCALE * (weighted_sum / partition[:, None] - pos_vec)
    delta_pooled = row_scale[:, None] * (
        delta_unit - unit_vec * jnp.sum(unit_vec * delta_unit, axis=1, keepdims=True)
    )
    delta_seq = (delta_pooled / LEN).astype(jnp.bfloat16)
    delta_row = lax.all_gather(delta_seq, "expert", axis=0, tiled=True)

    dims_t = (((0,), (0,)), ((), ()))
    spread_t = lax.optimization_barrier(lax.dot_general(
        weight_out[0], delta_row, (((1,), (1,)), ((), ())), preferred_element_type=jnp.float32
    ).astype(jnp.bfloat16))
    dhidden = lax.dot_general(
        sel_gate.astype(jnp.bfloat16), spread_t, (((0,), (1,)), ((), ())),
        preferred_element_type=jnp.float32,
    )
    delta_pre = lax.optimization_barrier((dhidden * slope_flat).astype(jnp.bfloat16))
    grad_in_term = lax.dot_general(
        input_flat, delta_pre, dims_t, preferred_element_type=jnp.float32
    ).astype(jnp.bfloat16)
    grad_out_term = lax.dot_general(
        seq_hidden.astype(jnp.bfloat16), delta_row, dims_t, preferred_element_type=jnp.float32
    ).astype(jnp.bfloat16)
    grad_in, grad_out = reduce_scatter_2d(
        grad_in_term, grad_out_term, nx, ny, lax.rem(dp_index, nx), dp_index // nx
    )
    return (grad_in[None], grad_out[None])


def solution(mesh):
    in_specs = (
        P(("dp", "expert"), None),
        P(("dp", "expert"), None),
        P(),
        P("expert", None, None),
        P("expert", None, None),
        P("dp", None),
        P(),
        P(),
    )
    out_specs = (P("expert", "dp", None), P("expert", "dp", None))
    return jax.shard_map(
        on_device, mesh=mesh, in_specs=in_specs, out_specs=out_specs, check_vma=False
    )
```

```python
import jax
import jax.numpy as jnp
from jax import lax
from jax.sharding import PartitionSpec as P

LEN = 64


SCORE_SCALE = 20.0
LOSS_SCALE = 64.0
EPSILON = 1e-06
HIGHEST = lax.Precision.HIGHEST


def gelu_parts(pre_act):
    inner_arg = 0.7978845608028654 * (pre_act + 0.044715 * pre_act * pre_act * pre_act)
    tangent = jnp.tanh(inner_arg)
    gelu_val = 0.5 * pre_act * (1.0 + tangent)
    slope_val = 0.5 * (1.0 + tangent) + 0.5 * pre_act * (
        1.0 - tangent * tangent
    ) * 0.7978845608028654 * (1.0 + 0.134145 * pre_act * pre_act)
    return (gelu_val, slope_val)


def route_slots(expert_ids, logits, experts, capacity):
    pick_hot = expert_ids[:, :, None] == jnp.arange(experts, dtype=jnp.int32)[None, None, :]
    picked = jnp.sum(jnp.where(pick_hot, logits[:, None, :], jnp.zeros((), logits.dtype)), axis=2)
    gate_wts = jax.nn.sigmoid(picked - picked[:, ::-1]).astype(jnp.bfloat16)
    flat_ids = expert_ids.reshape(-1)
    flat_hot = (flat_ids[:, None] == jnp.arange(experts, dtype=jnp.int32)[None, :]).astype(
        jnp.int32
    )
    running = jnp.cumsum(flat_hot, axis=0)
    position = jnp.sum(running * flat_hot, axis=1) - 1
    slot_ids = flat_ids * capacity + position
    return (gate_wts, slot_ids.reshape(expert_ids.shape))


def split_dot(a, b, dims):
    a_hi = a.astype(jnp.bfloat16)
    a_lo = (a - a_hi.astype(jnp.float32)).astype(jnp.bfloat16)
    hi = lax.dot_general(a_hi, b, dims, preferred_element_type=jnp.float32)
    lo = lax.dot_general(a_lo, b, dims, preferred_element_type=jnp.float32)
    return hi + lo


def contrast_terms(query_vec, key_rows, key_scale, open_mask, pos_hot):
    include = jnp.logical_or(open_mask, pos_hot)
    scores = (
        SCORE_SCALE
        * lax.dot_general(
            query_vec, key_rows, (((1,), (1,)), ((), ())), preferred_element_type=jnp.float32
        )
        * key_scale[None, :]
    )
    exp_scores = jnp.where(include, jnp.exp(scores), jnp.zeros((), scores.dtype))
    partition = jnp.sum(exp_scores, axis=1)
    soft_weight = (exp_scores * key_scale[None, :]).astype(jnp.bfloat16)
    weighted_sum = jnp.dot(soft_weight, key_rows, preferred_element_type=jnp.float32)
    pos_scale = jnp.sum(
        jnp.where(pos_hot, key_scale[None, :], jnp.zeros((), key_scale.dtype)), axis=1
    )
    pos_vec = (
        jnp.dot(pos_hot.astype(jnp.bfloat16), key_rows, preferred_element_type=jnp.float32)
        * pos_scale[:, None]
    )
    return (weighted_sum, partition, pos_vec)


def ring_pairs(nx, ny, along_x, step):
    pairs = []
    for y in range(ny):
        for x in range(nx):
            if along_x:
                pairs.append((y * nx + x, y * nx + (x + step) % nx))
            else:
                pairs.append((y * nx + x, ((y + step) % ny) * nx + x))
    return pairs


def take_chunk(chunks, index, count, axis=0):
    return lax.dynamic_index_in_dim(chunks, lax.rem(index + 2 * count, count), axis, keepdims=False)


def ring_start(fwd, bwd, count, pos, axis=0):
    return dict(fwd=fwd, bwd=bwd, count=count, pos=pos, axis=axis,
                acc_f=take_chunk(fwd, pos - 1, count, axis).astype(jnp.float32),
                acc_b=take_chunk(bwd, pos + 1, count, axis).astype(jnp.float32))


def ring_step(state, k, fwd_pairs, bwd_pairs):
    count, pos, axis = state["count"], state["pos"], state["axis"]
    got_f = lax.ppermute(state["acc_f"].astype(jnp.bfloat16), "dp", fwd_pairs)
    got_b = lax.ppermute(state["acc_b"].astype(jnp.bfloat16), "dp", bwd_pairs)
    state = dict(state)
    state["acc_f"] = got_f.astype(jnp.float32) + take_chunk(state["fwd"], pos - 2 - k, count, axis).astype(jnp.float32)
    state["acc_b"] = got_b.astype(jnp.float32) + take_chunk(state["bwd"], pos + 2 + k, count, axis).astype(jnp.float32)
    return state


def ring_stage(ra, rb, pairs_a, pairs_b):
    steps = ra["count"] - 1

    def body(k, carry):
        sa = dict(ra, acc_f=carry[0], acc_b=carry[1])
        sb = dict(rb, acc_f=carry[2], acc_b=carry[3])
        sa = ring_step(sa, k, *pairs_a)
        sb = ring_step(sb, k, *pairs_b)
        return (sa["acc_f"], sa["acc_b"], sb["acc_f"], sb["acc_b"])

    carry = lax.fori_loop(0, steps, body, (ra["acc_f"], ra["acc_b"], rb["acc_f"], rb["acc_b"]))
    return dict(ra, acc_f=carry[0], acc_b=carry[1]), dict(rb, acc_f=carry[2], acc_b=carry[3])


def reduce_scatter_2d(part_in, part_out, nx, ny, x_pos, y_pos):
    def grid(part):
        rows = part.shape[0] // (nx * ny)
        return part.reshape(ny, nx, rows, part.shape[1])

    gin, gout = grid(part_in), grid(part_out)
    hin, hout = gin.shape[-1] // 2, gout.shape[-1] // 2
    x_f, x_b = ring_pairs(nx, ny, True, 1), ring_pairs(nx, ny, True, -1)
    y_f, y_b = ring_pairs(nx, ny, False, 1), ring_pairs(nx, ny, False, -1)
    ra = ring_start(gin[..., :hin], gout[..., :hout], nx, x_pos, axis=1)
    rb = ring_start(gin[..., hin:], gout[..., hout:], ny, y_pos)
    ra, rb = ring_stage(ra, rb, (x_f, x_b), (y_f, y_b))
    ra = ring_start(ra["acc_f"], ra["acc_b"], ny, y_pos)
    rb = ring_start(rb["acc_f"], rb["acc_b"], nx, x_pos)
    ra, rb = ring_stage(ra, rb, (y_f, y_b), (x_f, x_b))
    total_in = jnp.concatenate([ra["acc_f"], rb["acc_f"]], axis=-1)
    total_out = jnp.concatenate([ra["acc_b"], rb["acc_b"]], axis=-1)
    return total_in, total_out


def on_device(tokens, expert_ids, router, weight_in, weight_out, premises, positive, tile_mask):
    token_count, model_width = tokens.shape
    ffn_width = weight_in.shape[2]
    experts = router.shape[1]
    expert_size = lax.axis_size("expert")
    dp_size = lax.axis_size("dp")
    nx = 4
    ny = dp_size // nx
    capacity = 4 * token_count // expert_size
    slot_total = experts * capacity
    seq_count = token_count // LEN
    row_seqs = expert_size * seq_count
    dp_index = lax.axis_index("dp")
    col_index = lax.axis_index("expert")
    device = dp_index * expert_size + col_index

    logits = jnp.dot(tokens, router, preferred_element_type=jnp.float32)
    gate_wts, slot_ids = route_slots(expert_ids, logits, experts, capacity)
    slot_hot = slot_ids[:, :, None] == jnp.arange(slot_total, dtype=jnp.int32)[None, None, :]
    placing = jnp.sum(slot_hot.astype(jnp.bfloat16), axis=1)
    combine = jnp.sum(
        jnp.where(slot_hot, gate_wts[:, :, None], jnp.zeros((), jnp.bfloat16)), axis=1
    )
    extra = 128
    seq_hot = (
        (jnp.arange(token_count, dtype=jnp.int32) // LEN)[:, None]
        == jnp.arange(extra, dtype=jnp.int32)[None, :]
    ).astype(jnp.bfloat16)
    payload = jnp.concatenate([tokens, seq_hot], axis=1)
    outgoing = lax.dot_general(
        placing, payload, (((0,), (0,)), ((), ())), preferred_element_type=jnp.float32
    )
    outgoing = jnp.concatenate(
        [outgoing[:, :model_width],
         lax.dot_general(combine, seq_hot, (((0,), (0,)), ((), ())),
                         preferred_element_type=jnp.float32)],
        axis=1,
    ).astype(jnp.bfloat16)
    outgoing = outgoing.reshape(experts, capacity, model_width + extra)
    arrived = lax.all_to_all(outgoing, "expert", split_axis=0, concat_axis=0, tiled=True)
    input_flat = arrived[:, :, :model_width].reshape(expert_size * capacity, model_width)
    my_meta = arrived[:, :, model_width:model_width + seq_count].astype(jnp.float32)
    same_src = jnp.eye(expert_size, dtype=jnp.float32)
    meta_t = jnp.transpose(my_meta, (2, 0, 1))
    sel_gate = same_src[:, None, :, None] * meta_t[None, :, :, :]
    sel_gate = sel_gate.reshape(row_seqs, expert_size * capacity)

    pre_act = jnp.dot(input_flat, weight_in[0], preferred_element_type=jnp.float32)
    gelu_val, slope_flat = gelu_parts(pre_act)
    hidden = gelu_val.astype(jnp.bfloat16)
    seq_hidden = jnp.dot(sel_gate.astype(jnp.bfloat16), hidden, preferred_element_type=jnp.float32)
    moe_seq = split_dot(seq_hidden, weight_out[0], (((1,), (0,)), ((), ())))
    moe_back = lax.all_to_all(
        moe_seq.reshape(expert_size, seq_count, model_width), "expert",
        split_axis=0, concat_axis=0, tiled=True,
    )
    moe_mine = jnp.sum(moe_back, axis=0)

    token_sum = jnp.sum(tokens.astype(jnp.float32).reshape(seq_count, LEN, model_width), axis=1)
    pooled = (token_sum + moe_mine) / LEN
    row_scale = lax.rsqrt(jnp.sum(pooled * pooled, axis=1) + EPSILON)
    unit_vec = pooled * row_scale[:, None]
    query_vec = unit_vec.astype(jnp.bfloat16)
    prem_count = premises.shape[0]
    key_rows = lax.all_gather(premises, "dp", axis=0, tiled=True)
    key_scale = lax.rsqrt(jnp.sum(jnp.square(key_rows.astype(jnp.float32)), axis=1) + EPSILON)
    key_index = jnp.arange(key_rows.shape[0], dtype=jnp.int32)
    own_positive = lax.dynamic_slice_in_dim(positive, device * seq_count, seq_count)
    mask_row = lax.dynamic_index_in_dim(tile_mask, device, 0, keepdims=False)
    key_open = jnp.repeat(mask_row, prem_count) == 1
    weighted_sum, partition, pos_vec = contrast_terms(
        query_vec,
        key_rows,
        key_scale,
        key_open[None, :],
        key_index[None, :] == own_positive[:, None],
    )
    delta_unit = LOSS_SCALE * SCORE_SCALE * (weighted_sum / partition[:, None] - pos_vec)
    delta_pooled = row_scale[:, None] * (
        delta_unit - unit_vec * jnp.sum(unit_vec * delta_unit, axis=1, keepdims=True)
    )
    delta_seq = (delta_pooled / LEN).astype(jnp.bfloat16)
    delta_row = lax.all_gather(delta_seq, "expert", axis=0, tiled=True)

    dims_t = (((0,), (0,)), ((), ()))
    spread_t = lax.optimization_barrier(lax.dot_general(
        weight_out[0], delta_row, (((1,), (1,)), ((), ())), preferred_element_type=jnp.float32
    ).astype(jnp.bfloat16))
    dhidden = lax.dot_general(
        sel_gate.astype(jnp.bfloat16), spread_t, (((0,), (1,)), ((), ())),
        preferred_element_type=jnp.float32,
    )
    delta_pre = lax.optimization_barrier((dhidden * slope_flat).astype(jnp.bfloat16))
    grad_in_term = lax.dot_general(
        input_flat, delta_pre, dims_t, preferred_element_type=jnp.float32
    ).astype(jnp.bfloat16)
    grad_out_term = lax.dot_general(
        seq_hidden.astype(jnp.bfloat16), delta_row, dims_t, preferred_element_type=jnp.float32
    ).astype(jnp.bfloat16)
    grad_in, grad_out = reduce_scatter_2d(
        grad_in_term, grad_out_term, nx, ny, lax.rem(dp_index, nx), dp_index // nx
    )
    return (grad_in[None], grad_out[None])


def solution(mesh):
    in_specs = (
        P(("dp", "expert"), None),
        P(("dp", "expert"), None),
        P(),
        P("expert", None, None),
        P("expert", None, None),
        P("dp", None),
        P(),
        P(),
    )
    out_specs = (P("expert", "dp", None), P("expert", "dp", None))
    return jax.shard_map(
        on_device, mesh=mesh, in_specs=in_specs, out_specs=out_specs, check_vma=False
    )
```

```python
import jax
import jax.numpy as jnp
from jax import lax
from jax.sharding import PartitionSpec as P


LEN = 64


SCORE_SCALE = 20.0
LOSS_SCALE = 64.0
EPSILON = 1e-06


def gelu_parts(pre_act):
    inner_arg = 0.7978845608028654 * (pre_act + 0.044715 * pre_act * pre_act * pre_act)
    tangent = jnp.tanh(inner_arg)
    gelu_val = 0.5 * pre_act * (1.0 + tangent)
    slope_val = 0.5 * (1.0 + tangent) + 0.5 * pre_act * (
        1.0 - tangent * tangent
    ) * 0.7978845608028654 * (1.0 + 0.134145 * pre_act * pre_act)
    return (gelu_val, slope_val)


def route_slots(expert_ids, logits, experts, capacity):
    pick_hot = expert_ids[:, :, None] == jnp.arange(experts, dtype=jnp.int32)[None, None, :]
    picked = jnp.sum(jnp.where(pick_hot, logits[:, None, :], jnp.zeros((), logits.dtype)), axis=2)
    gate_wts = jax.nn.sigmoid(picked - picked[:, ::-1]).astype(jnp.bfloat16)
    flat_ids = expert_ids.reshape(-1)
    flat_hot = (flat_ids[:, None] == jnp.arange(experts, dtype=jnp.int32)[None, :]).astype(
        jnp.int32
    )
    running = jnp.cumsum(flat_hot, axis=0)
    position = jnp.sum(running * flat_hot, axis=1) - 1
    slot_ids = flat_ids * capacity + position
    return (gate_wts, slot_ids.reshape(expert_ids.shape))


def split_dot(a, b, dims):
    a_hi = a.astype(jnp.bfloat16)
    a_lo = (a - a_hi.astype(jnp.float32)).astype(jnp.bfloat16)
    hi = lax.dot_general(a_hi, b, dims, preferred_element_type=jnp.float32)
    lo = lax.dot_general(a_lo, b, dims, preferred_element_type=jnp.float32)
    return hi + lo


def contrast_terms(query_vec, key_rows, key_scale, open_mask, pos_hot):
    include = jnp.logical_or(open_mask, pos_hot)
    scores = (
        SCORE_SCALE
        * lax.dot_general(
            query_vec, key_rows, (((1,), (1,)), ((), ())), preferred_element_type=jnp.float32
        )
        * key_scale[None, :]
    )
    exp_scores = jnp.where(include, jnp.exp(scores), jnp.zeros((), scores.dtype))
    partition = jnp.sum(exp_scores, axis=1)
    soft_weight = (exp_scores * key_scale[None, :]).astype(jnp.bfloat16)
    weighted_sum = jnp.dot(soft_weight, key_rows, preferred_element_type=jnp.float32)
    pos_scale = jnp.sum(
        jnp.where(pos_hot, key_scale[None, :], jnp.zeros((), key_scale.dtype)), axis=1
    )
    pos_vec = (
        jnp.dot(pos_hot.astype(jnp.bfloat16), key_rows, preferred_element_type=jnp.float32)
        * pos_scale[:, None]
    )
    return (weighted_sum, partition, pos_vec)


def ring_pairs(nx, ny, along_x, step):
    pairs = []
    for y in range(ny):
        for x in range(nx):
            if along_x:
                pairs.append((y * nx + x, y * nx + (x + step) % nx))
            else:
                pairs.append((y * nx + x, ((y + step) % ny) * nx + x))
    return pairs


def take_chunk(chunks, index, count, axis=0):
    return lax.dynamic_index_in_dim(chunks, lax.rem(index + 2 * count, count), axis, keepdims=False)


def ring_start(fwd, bwd, count, pos, axis=0):
    return dict(fwd=fwd, bwd=bwd, count=count, pos=pos, axis=axis,
                acc_f=take_chunk(fwd, pos - 1, count, axis).astype(jnp.float32),
                acc_b=take_chunk(bwd, pos + 1, count, axis).astype(jnp.float32))


def ring_step(state, k, fwd_pairs, bwd_pairs):
    count, pos, axis = state["count"], state["pos"], state["axis"]
    got_f = lax.ppermute(state["acc_f"].astype(jnp.bfloat16), "dp", fwd_pairs)
    got_b = lax.ppermute(state["acc_b"].astype(jnp.bfloat16), "dp", bwd_pairs)
    state = dict(state)
    state["acc_f"] = got_f.astype(jnp.float32) + take_chunk(state["fwd"], pos - 2 - k, count, axis).astype(jnp.float32)
    state["acc_b"] = got_b.astype(jnp.float32) + take_chunk(state["bwd"], pos + 2 + k, count, axis).astype(jnp.float32)
    return state


def reduce_scatter_2d(part_in, part_out, nx, ny, x_pos, y_pos):
    def grid(part):
        rows = part.shape[0] // (nx * ny)
        return part.reshape(ny, nx, rows, part.shape[1])

    gin, gout = grid(part_in), grid(part_out)
    hin, hout = gin.shape[-1] // 2, gout.shape[-1] // 2
    x_f, x_b = ring_pairs(nx, ny, True, 1), ring_pairs(nx, ny, True, -1)
    y_f, y_b = ring_pairs(nx, ny, False, 1), ring_pairs(nx, ny, False, -1)
    ra = ring_start(gin[..., :hin], gout[..., :hout], nx, x_pos, axis=1)
    rb = ring_start(gin[..., hin:], gout[..., hout:], ny, y_pos)
    for k in range(max(nx, ny) - 1):
        if k < nx - 1:
            ra = ring_step(ra, k, x_f, x_b)
        if k < ny - 1:
            rb = ring_step(rb, k, y_f, y_b)
    ra = ring_start(ra["acc_f"], ra["acc_b"], ny, y_pos)
    rb = ring_start(rb["acc_f"], rb["acc_b"], nx, x_pos)
    for k in range(max(nx, ny) - 1):
        if k < ny - 1:
            ra = ring_step(ra, k, y_f, y_b)
        if k < nx - 1:
            rb = ring_step(rb, k, x_f, x_b)
    total_in = jnp.concatenate([ra["acc_f"], rb["acc_f"]], axis=-1)
    total_out = jnp.concatenate([ra["acc_b"], rb["acc_b"]], axis=-1)
    return total_in, total_out


def device_body(tokens, expert_ids, router, weight_in, weight_out, premises, positive, tile_mask):
    token_count, model_width = tokens.shape
    experts = router.shape[1]
    expert_size = lax.axis_size("expert")
    dp_size = lax.axis_size("dp")
    nx = 4
    ny = dp_size // nx
    capacity = 4 * token_count // expert_size
    slot_total = experts * capacity
    seq_count = token_count // LEN
    row_seqs = expert_size * seq_count
    dp_index = lax.axis_index("dp")
    col_index = lax.axis_index("expert")
    device = dp_index * expert_size + col_index

    logits = jnp.dot(tokens, router, preferred_element_type=jnp.float32)
    gate_wts, slot_ids = route_slots(expert_ids, logits, experts, capacity)
    slot_hot = slot_ids[:, :, None] == jnp.arange(slot_total, dtype=jnp.int32)[None, None, :]
    placing = jnp.sum(slot_hot.astype(jnp.bfloat16), axis=1)
    combine = jnp.sum(
        jnp.where(slot_hot, gate_wts[:, :, None], jnp.zeros((), jnp.bfloat16)), axis=1
    )
    extra = 128
    seq_hot = (
        (jnp.arange(token_count, dtype=jnp.int32) // LEN)[:, None]
        == jnp.arange(extra, dtype=jnp.int32)[None, :]
    ).astype(jnp.bfloat16)
    payload = jnp.concatenate([tokens, seq_hot], axis=1)
    outgoing = lax.dot_general(
        placing, payload, (((0,), (0,)), ((), ())), preferred_element_type=jnp.float32
    )
    outgoing = jnp.concatenate(
        [outgoing[:, :model_width],
         lax.dot_general(combine, seq_hot, (((0,), (0,)), ((), ())),
                         preferred_element_type=jnp.float32)],
        axis=1,
    ).astype(jnp.bfloat16)
    outgoing = outgoing.reshape(experts, capacity, model_width + extra)
    arrived = lax.all_to_all(outgoing, "expert", split_axis=0, concat_axis=0, tiled=True)
    input_flat = arrived[:, :, :model_width].reshape(expert_size * capacity, model_width)
    my_meta = arrived[:, :, model_width:model_width + seq_count].astype(jnp.float32)
    same_src = jnp.eye(expert_size, dtype=jnp.float32)
    meta_t = jnp.transpose(my_meta, (2, 0, 1))
    sel_gate = same_src[:, None, :, None] * meta_t[None, :, :, :]
    sel_gate = sel_gate.reshape(row_seqs, expert_size * capacity)

    pre_act = jnp.dot(input_flat, weight_in[0], preferred_element_type=jnp.float32)
    gelu_val, slope_flat = gelu_parts(pre_act)
    hidden = gelu_val.astype(jnp.bfloat16)
    seq_hidden = jnp.dot(sel_gate.astype(jnp.bfloat16), hidden, preferred_element_type=jnp.float32)
    moe_seq = split_dot(seq_hidden, weight_out[0], (((1,), (0,)), ((), ())))
    moe_back = lax.all_to_all(
        moe_seq.reshape(expert_size, seq_count, model_width), "expert",
        split_axis=0, concat_axis=0, tiled=True,
    )
    moe_mine = jnp.sum(moe_back, axis=0)

    token_sum = jnp.sum(tokens.astype(jnp.float32).reshape(seq_count, LEN, model_width), axis=1)
    pooled = (token_sum + moe_mine) / LEN
    row_scale = lax.rsqrt(jnp.sum(pooled * pooled, axis=1) + EPSILON)
    unit_vec = pooled * row_scale[:, None]
    query_vec = unit_vec.astype(jnp.bfloat16)
    prem_count = premises.shape[0]
    key_rows = lax.all_gather(premises, "dp", axis=0, tiled=True)
    key_scale = lax.rsqrt(jnp.sum(jnp.square(key_rows.astype(jnp.float32)), axis=1) + EPSILON)
    key_index = jnp.arange(key_rows.shape[0], dtype=jnp.int32)
    own_positive = lax.dynamic_slice_in_dim(positive, device * seq_count, seq_count)
    mask_row = lax.dynamic_index_in_dim(tile_mask, device, 0, keepdims=False)
    key_open = jnp.repeat(mask_row, prem_count) == 1
    weighted_sum, partition, pos_vec = contrast_terms(
        query_vec,
        key_rows,
        key_scale,
        key_open[None, :],
        key_index[None, :] == own_positive[:, None],
    )
    delta_unit = LOSS_SCALE * SCORE_SCALE * (weighted_sum / partition[:, None] - pos_vec)
    delta_pooled = row_scale[:, None] * (
        delta_unit - unit_vec * jnp.sum(unit_vec * delta_unit, axis=1, keepdims=True)
    )
    delta_seq = (delta_pooled / LEN).astype(jnp.bfloat16)
    delta_row = lax.all_gather(delta_seq, "expert", axis=0, tiled=True)

    dims_t = (((0,), (0,)), ((), ()))
    spread_t = lax.optimization_barrier(lax.dot_general(
        weight_out[0], delta_row, (((1,), (1,)), ((), ())), preferred_element_type=jnp.float32
    ).astype(jnp.bfloat16))
    dhidden = lax.dot_general(
        sel_gate.astype(jnp.bfloat16), spread_t, (((0,), (1,)), ((), ())),
        preferred_element_type=jnp.float32,
    )
    delta_pre = lax.optimization_barrier((dhidden * slope_flat).astype(jnp.bfloat16))
    grad_in_term = lax.dot_general(
        input_flat, delta_pre, dims_t, preferred_element_type=jnp.float32
    ).astype(jnp.bfloat16)
    grad_out_term = lax.dot_general(
        seq_hidden.astype(jnp.bfloat16), delta_row, dims_t, preferred_element_type=jnp.float32
    ).astype(jnp.bfloat16)
    grad_in, grad_out = reduce_scatter_2d(
        grad_in_term, grad_out_term, nx, ny, lax.rem(dp_index, nx), dp_index // nx
    )
    return (grad_in[None], grad_out[None])


def solution(mesh):
    in_specs = (
        P(("dp", "expert"), None),
        P(("dp", "expert"), None),
        P(),
        P("expert", None, None),
        P("expert", None, None),
        P("dp", None),
        P(),
        P(),
    )
    out_specs = (P("expert", "dp", None), P("expert", "dp", None))
    return jax.shard_map(
        device_body, mesh=mesh, in_specs=in_specs, out_specs=out_specs, check_vma=False
    )
```

```python
import jax
import jax.numpy as jnp
from jax import lax
from jax.sharding import PartitionSpec as P

LEN = 64


SCORE_SCALE = 20.0
LOSS_SCALE = 64.0
EPSILON = 1e-06
HIGHEST = lax.Precision.HIGHEST


def gelu_parts(pre_act):
    inner_arg = 0.7978845608028654 * (pre_act + 0.044715 * pre_act * pre_act * pre_act)
    tangent = jnp.tanh(inner_arg)
    gelu_val = 0.5 * pre_act * (1.0 + tangent)
    slope_val = 0.5 * (1.0 + tangent) + 0.5 * pre_act * (
        1.0 - tangent * tangent
    ) * 0.7978845608028654 * (1.0 + 0.134145 * pre_act * pre_act)
    return (gelu_val, slope_val)


def route_slots(expert_ids, logits, experts, capacity):
    pick_hot = expert_ids[:, :, None] == jnp.arange(experts, dtype=jnp.int32)[None, None, :]
    picked = jnp.sum(jnp.where(pick_hot, logits[:, None, :], jnp.zeros((), logits.dtype)), axis=2)
    gate_wts = jax.nn.sigmoid(picked - picked[:, ::-1]).astype(jnp.bfloat16)
    flat_ids = expert_ids.reshape(-1)
    flat_hot = (flat_ids[:, None] == jnp.arange(experts, dtype=jnp.int32)[None, :]).astype(
        jnp.int32
    )
    running = jnp.cumsum(flat_hot, axis=0)
    position = jnp.sum(running * flat_hot, axis=1) - 1
    slot_ids = flat_ids * capacity + position
    return (gate_wts, slot_ids.reshape(expert_ids.shape))


def split_dot(a, b, dims):
    a_hi = a.astype(jnp.bfloat16)
    a_lo = (a - a_hi.astype(jnp.float32)).astype(jnp.bfloat16)
    hi = lax.dot_general(a_hi, b, dims, preferred_element_type=jnp.float32)
    lo = lax.dot_general(a_lo, b, dims, preferred_element_type=jnp.float32)
    return hi + lo


def contrast_terms(query_vec, key_rows, key_scale, open_mask, pos_hot):
    include = jnp.logical_or(open_mask, pos_hot)
    scores = (
        SCORE_SCALE
        * lax.dot_general(
            query_vec, key_rows, (((1,), (1,)), ((), ())), preferred_element_type=jnp.float32
        )
        * key_scale[None, :]
    )
    exp_scores = jnp.where(include, jnp.exp(scores), jnp.zeros((), scores.dtype))
    partition = jnp.sum(exp_scores, axis=1)
    soft_weight = (exp_scores * key_scale[None, :]).astype(jnp.bfloat16)
    weighted_sum = jnp.dot(soft_weight, key_rows, preferred_element_type=jnp.float32)
    pos_scale = jnp.sum(
        jnp.where(pos_hot, key_scale[None, :], jnp.zeros((), key_scale.dtype)), axis=1
    )
    pos_vec = (
        jnp.dot(pos_hot.astype(jnp.bfloat16), key_rows, preferred_element_type=jnp.float32)
        * pos_scale[:, None]
    )
    return (weighted_sum, partition, pos_vec)


def ring_pairs(nx, ny, along_x, step):
    pairs = []
    for y in range(ny):
        for x in range(nx):
            if along_x:
                pairs.append((y * nx + x, y * nx + (x + step) % nx))
            else:
                pairs.append((y * nx + x, ((y + step) % ny) * nx + x))
    return pairs


def take_chunk(chunks, index, count, axis=0):
    return lax.dynamic_index_in_dim(chunks, lax.rem(index + 2 * count, count), axis, keepdims=False)


def ring_start(fwd, bwd, count, pos, axis=0):
    return dict(fwd=fwd, bwd=bwd, count=count, pos=pos, axis=axis,
                acc_f=take_chunk(fwd, pos - 1, count, axis).astype(jnp.float32),
                acc_b=take_chunk(bwd, pos + 1, count, axis).astype(jnp.float32))


def ring_step(state, k, fwd_pairs, bwd_pairs):
    count, pos, axis = state["count"], state["pos"], state["axis"]
    got_f = lax.ppermute(state["acc_f"].astype(jnp.bfloat16), "dp", fwd_pairs)
    got_b = lax.ppermute(state["acc_b"].astype(jnp.bfloat16), "dp", bwd_pairs)
    state = dict(state)
    state["acc_f"] = got_f.astype(jnp.float32) + take_chunk(state["fwd"], pos - 2 - k, count, axis).astype(jnp.float32)
    state["acc_b"] = got_b.astype(jnp.float32) + take_chunk(state["bwd"], pos + 2 + k, count, axis).astype(jnp.float32)
    return state


def reduce_scatter_2d(part_in, part_out, nx, ny, x_pos, y_pos):
    def grid(part):
        rows = part.shape[0] // (nx * ny)
        return part.reshape(ny, nx, rows, part.shape[1])

    gin, gout = grid(part_in), grid(part_out)
    hin, hout = gin.shape[-1] // 2, gout.shape[-1] // 2
    x_f, x_b = ring_pairs(nx, ny, True, 1), ring_pairs(nx, ny, True, -1)
    y_f, y_b = ring_pairs(nx, ny, False, 1), ring_pairs(nx, ny, False, -1)
    ra = ring_start(gin[..., :hin], gout[..., :hout], nx, x_pos, axis=1)
    rb = ring_start(gin[..., hin:], gout[..., hout:], ny, y_pos)
    for k in range(max(nx, ny) - 1):
        if k < nx - 1:
            ra = ring_step(ra, k, x_f, x_b)
        if k < ny - 1:
            rb = ring_step(rb, k, y_f, y_b)
    ra = ring_start(ra["acc_f"], ra["acc_b"], ny, y_pos)
    rb = ring_start(rb["acc_f"], rb["acc_b"], nx, x_pos)
    for k in range(max(nx, ny) - 1):
        if k < ny - 1:
            ra = ring_step(ra, k, y_f, y_b)
        if k < nx - 1:
            rb = ring_step(rb, k, x_f, x_b)
    total_in = jnp.concatenate([ra["acc_f"], rb["acc_f"]], axis=-1)
    total_out = jnp.concatenate([ra["acc_b"], rb["acc_b"]], axis=-1)
    return total_in, total_out


def on_device(tokens, expert_ids, router, weight_in, weight_out, premises, positive, tile_mask):
    token_count, model_width = tokens.shape
    ffn_width = weight_in.shape[2]
    experts = router.shape[1]
    expert_size = lax.axis_size("expert")
    dp_size = lax.axis_size("dp")
    nx = 4
    ny = dp_size // nx
    capacity = 4 * token_count // expert_size
    slot_total = experts * capacity
    seq_count = token_count // LEN
    row_seqs = expert_size * seq_count
    dp_index = lax.axis_index("dp")
    col_index = lax.axis_index("expert")
    device = dp_index * expert_size + col_index

    logits = jnp.dot(tokens, router, preferred_element_type=jnp.float32)
    gate_wts, slot_ids = route_slots(expert_ids, logits, experts, capacity)
    slot_hot = slot_ids[:, :, None] == jnp.arange(slot_total, dtype=jnp.int32)[None, None, :]
    placing = jnp.sum(slot_hot.astype(jnp.bfloat16), axis=1)
    combine = jnp.sum(
        jnp.where(slot_hot, gate_wts[:, :, None], jnp.zeros((), jnp.bfloat16)), axis=1
    )
    extra = 128
    seq_hot = (
        (jnp.arange(token_count, dtype=jnp.int32) // LEN)[:, None]
        == jnp.arange(extra, dtype=jnp.int32)[None, :]
    ).astype(jnp.bfloat16)
    payload = jnp.concatenate([tokens, seq_hot], axis=1)
    outgoing = lax.dot_general(
        placing, payload, (((0,), (0,)), ((), ())), preferred_element_type=jnp.float32
    )
    outgoing = jnp.concatenate(
        [outgoing[:, :model_width],
         lax.dot_general(combine, seq_hot, (((0,), (0,)), ((), ())),
                         preferred_element_type=jnp.float32)],
        axis=1,
    ).astype(jnp.bfloat16)
    outgoing = outgoing.reshape(experts, capacity, model_width + extra)
    arrived = lax.all_to_all(outgoing, "expert", split_axis=0, concat_axis=0, tiled=True)
    input_flat = arrived[:, :, :model_width].reshape(expert_size * capacity, model_width)
    my_meta = arrived[:, :, model_width:model_width + seq_count].astype(jnp.float32)
    same_src = jnp.eye(expert_size, dtype=jnp.float32)
    meta_t = jnp.transpose(my_meta, (2, 0, 1))
    sel_gate = same_src[:, None, :, None] * meta_t[None, :, :, :]
    sel_gate = sel_gate.reshape(row_seqs, expert_size * capacity)

    pre_act = jnp.dot(input_flat, weight_in[0], preferred_element_type=jnp.float32)
    gelu_val, slope_flat = gelu_parts(pre_act)
    hidden = gelu_val.astype(jnp.bfloat16)
    seq_hidden = jnp.dot(sel_gate.astype(jnp.bfloat16), hidden, preferred_element_type=jnp.float32)
    moe_seq = split_dot(seq_hidden, weight_out[0], (((1,), (0,)), ((), ())))
    moe_back = lax.all_to_all(
        moe_seq.reshape(expert_size, seq_count, model_width), "expert",
        split_axis=0, concat_axis=0, tiled=True,
    )
    moe_mine = jnp.sum(moe_back, axis=0)

    token_sum = jnp.sum(tokens.astype(jnp.float32).reshape(seq_count, LEN, model_width), axis=1)
    pooled = (token_sum + moe_mine) / LEN
    row_scale = lax.rsqrt(jnp.sum(pooled * pooled, axis=1) + EPSILON)
    unit_vec = pooled * row_scale[:, None]
    query_vec = unit_vec.astype(jnp.bfloat16)
    prem_count = premises.shape[0]
    key_rows = lax.all_gather(premises, "dp", axis=0, tiled=True)
    key_scale = lax.rsqrt(jnp.sum(jnp.square(key_rows.astype(jnp.float32)), axis=1) + EPSILON)
    key_index = jnp.arange(key_rows.shape[0], dtype=jnp.int32)
    own_positive = lax.dynamic_slice_in_dim(positive, device * seq_count, seq_count)
    mask_row = lax.dynamic_index_in_dim(tile_mask, device, 0, keepdims=False)
    key_open = jnp.repeat(mask_row, prem_count) == 1
    weighted_sum, partition, pos_vec = contrast_terms(
        query_vec,
        key_rows,
        key_scale,
        key_open[None, :],
        key_index[None, :] == own_positive[:, None],
    )
    delta_unit = LOSS_SCALE * SCORE_SCALE * (weighted_sum / partition[:, None] - pos_vec)
    delta_pooled = row_scale[:, None] * (
        delta_unit - unit_vec * jnp.sum(unit_vec * delta_unit, axis=1, keepdims=True)
    )
    delta_seq = (delta_pooled / LEN).astype(jnp.bfloat16)
    delta_row = lax.all_to_all(
        jnp.broadcast_to(delta_seq[None], (expert_size,) + delta_seq.shape), "expert",
        split_axis=0, concat_axis=0, tiled=True,
    ).reshape(row_seqs, model_width)

    dims_t = (((0,), (0,)), ((), ()))
    spread_t = lax.optimization_barrier(lax.dot_general(
        weight_out[0], delta_row, (((1,), (1,)), ((), ())), preferred_element_type=jnp.float32
    ).astype(jnp.bfloat16))
    dhidden = lax.dot_general(
        sel_gate.astype(jnp.bfloat16), spread_t, (((0,), (1,)), ((), ())),
        preferred_element_type=jnp.float32,
    )
    delta_pre = lax.optimization_barrier((dhidden * slope_flat).astype(jnp.bfloat16))
    grad_in_term = lax.dot_general(
        input_flat, delta_pre, dims_t, preferred_element_type=jnp.float32
    ).astype(jnp.bfloat16)
    grad_out_term = lax.dot_general(
        seq_hidden.astype(jnp.bfloat16), delta_row, dims_t, preferred_element_type=jnp.float32
    ).astype(jnp.bfloat16)
    grad_in, grad_out = reduce_scatter_2d(
        grad_in_term, grad_out_term, nx, ny, lax.rem(dp_index, nx), dp_index // nx
    )
    return (grad_in[None], grad_out[None])


def solution(mesh):
    in_specs = (
        P(("dp", "expert"), None),
        P(("dp", "expert"), None),
        P(),
        P("expert", None, None),
        P("expert", None, None),
        P("dp", None),
        P(),
        P(),
    )
    out_specs = (P("expert", "dp", None), P("expert", "dp", None))
    return jax.shard_map(
        on_device, mesh=mesh, in_specs=in_specs, out_specs=out_specs, check_vma=False
    )
```

```python
import jax
import jax.numpy as jnp
from jax import lax
from jax.sharding import PartitionSpec as P

LEN = 64


SCORE_SCALE = 20.0
LOSS_SCALE = 64.0
EPSILON = 1e-06
HIGHEST = lax.Precision.HIGHEST


def gelu_parts(pre_act):
    inner_arg = 0.7978845608028654 * (pre_act + 0.044715 * pre_act * pre_act * pre_act)
    tangent = jnp.tanh(inner_arg)
    gelu_val = 0.5 * pre_act * (1.0 + tangent)
    slope_val = 0.5 * (1.0 + tangent) + 0.5 * pre_act * (
        1.0 - tangent * tangent
    ) * 0.7978845608028654 * (1.0 + 0.134145 * pre_act * pre_act)
    return (gelu_val, slope_val)


def route_slots(expert_ids, logits, experts, capacity):
    pick_hot = expert_ids[:, :, None] == jnp.arange(experts, dtype=jnp.int32)[None, None, :]
    picked = jnp.sum(jnp.where(pick_hot, logits[:, None, :], jnp.zeros((), logits.dtype)), axis=2)
    gate_wts = jax.nn.sigmoid(picked - picked[:, ::-1]).astype(jnp.bfloat16)
    flat_ids = expert_ids.reshape(-1)
    flat_hot = (flat_ids[:, None] == jnp.arange(experts, dtype=jnp.int32)[None, :]).astype(
        jnp.int32
    )
    running = jnp.cumsum(flat_hot, axis=0)
    position = jnp.sum(running * flat_hot, axis=1) - 1
    slot_ids = flat_ids * capacity + position
    return (gate_wts, slot_ids.reshape(expert_ids.shape))


def split_dot(a, b, dims):
    a_hi = a.astype(jnp.bfloat16)
    a_lo = (a - a_hi.astype(jnp.float32)).astype(jnp.bfloat16)
    hi = lax.dot_general(a_hi, b, dims, preferred_element_type=jnp.float32)
    lo = lax.dot_general(a_lo, b, dims, preferred_element_type=jnp.float32)
    return hi + lo


def contrast_terms(query_vec, key_rows, key_scale, open_mask, pos_hot):
    include = jnp.logical_or(open_mask, pos_hot)
    scores = (
        SCORE_SCALE
        * lax.dot_general(
            query_vec, key_rows, (((1,), (1,)), ((), ())), preferred_element_type=jnp.float32
        )
        * key_scale[None, :]
    )
    exp_scores = jnp.where(include, jnp.exp(scores), jnp.zeros((), scores.dtype))
    partition = jnp.sum(exp_scores, axis=1)
    soft_weight = (exp_scores * key_scale[None, :]).astype(jnp.bfloat16)
    weighted_sum = jnp.dot(soft_weight, key_rows, preferred_element_type=jnp.float32)
    pos_scale = jnp.sum(
        jnp.where(pos_hot, key_scale[None, :], jnp.zeros((), key_scale.dtype)), axis=1
    )
    pos_vec = (
        jnp.dot(pos_hot.astype(jnp.bfloat16), key_rows, preferred_element_type=jnp.float32)
        * pos_scale[:, None]
    )
    return (weighted_sum, partition, pos_vec)


def ring_pairs(nx, ny, along_x, step):
    pairs = []
    for y in range(ny):
        for x in range(nx):
            if along_x:
                pairs.append((y * nx + x, y * nx + (x + step) % nx))
            else:
                pairs.append((y * nx + x, ((y + step) % ny) * nx + x))
    return pairs


def take_chunk(chunks, index, count, axis=0):
    return lax.dynamic_index_in_dim(chunks, lax.rem(index + 2 * count, count), axis, keepdims=False)


def ring_start(fwd, bwd, count, pos, axis=0):
    return dict(fwd=fwd, bwd=bwd, count=count, pos=pos, axis=axis,
                acc_f=take_chunk(fwd, pos - 1, count, axis).astype(jnp.float32),
                acc_b=take_chunk(bwd, pos + 1, count, axis).astype(jnp.float32))


def ring_step(state, k, fwd_pairs, bwd_pairs):
    count, pos, axis = state["count"], state["pos"], state["axis"]
    got_f = lax.ppermute(state["acc_f"].astype(jnp.bfloat16), "dp", fwd_pairs)
    got_b = lax.ppermute(state["acc_b"].astype(jnp.bfloat16), "dp", bwd_pairs)
    state = dict(state)
    state["acc_f"] = got_f.astype(jnp.float32) + take_chunk(state["fwd"], pos - 2 - k, count, axis).astype(jnp.float32)
    state["acc_b"] = got_b.astype(jnp.float32) + take_chunk(state["bwd"], pos + 2 + k, count, axis).astype(jnp.float32)
    return state


def reduce_scatter_2d(part_in, part_out, nx, ny, x_pos, y_pos):
    def grid(part):
        rows = part.shape[0] // (nx * ny)
        return part.reshape(ny, nx, rows, part.shape[1])

    gin, gout = grid(part_in), grid(part_out)
    hin, hout = gin.shape[-1] // 2, gout.shape[-1] // 2
    x_f, x_b = ring_pairs(nx, ny, True, 1), ring_pairs(nx, ny, True, -1)
    y_f, y_b = ring_pairs(nx, ny, False, 1), ring_pairs(nx, ny, False, -1)
    ra = ring_start(gin[..., :hin], gout[..., :hout], nx, x_pos, axis=1)
    rb = ring_start(gin[..., hin:], gout[..., hout:], ny, y_pos)
    for k in range(max(nx, ny) - 1):
        if k < nx - 1:
            ra = ring_step(ra, k, x_f, x_b)
        if k < ny - 1:
            rb = ring_step(rb, k, y_f, y_b)
    ra = ring_start(ra["acc_f"], ra["acc_b"], ny, y_pos)
    rb = ring_start(rb["acc_f"], rb["acc_b"], nx, x_pos)
    for k in range(max(nx, ny) - 1):
        if k < ny - 1:
            ra = ring_step(ra, k, y_f, y_b)
        if k < nx - 1:
            rb = ring_step(rb, k, x_f, x_b)
    total_in = jnp.concatenate([ra["acc_f"], rb["acc_f"]], axis=-1)
    total_out = jnp.concatenate([ra["acc_b"], rb["acc_b"]], axis=-1)
    return total_in, total_out


def on_device(tokens, expert_ids, router, weight_in, weight_out, premises, positive, tile_mask):
    token_count, model_width = tokens.shape
    ffn_width = weight_in.shape[2]
    experts = router.shape[1]
    expert_size = lax.axis_size("expert")
    dp_size = lax.axis_size("dp")
    nx = 4
    ny = dp_size // nx
    capacity = 4 * token_count // expert_size
    slot_total = experts * capacity
    seq_count = token_count // LEN
    row_seqs = expert_size * seq_count
    dp_index = lax.axis_index("dp")
    col_index = lax.axis_index("expert")
    device = dp_index * expert_size + col_index

    logits = jnp.dot(tokens, router, preferred_element_type=jnp.float32)
    gate_wts, slot_ids = route_slots(expert_ids, logits, experts, capacity)
    slot_hot = slot_ids[:, :, None] == jnp.arange(slot_total, dtype=jnp.int32)[None, None, :]
    placing = jnp.sum(slot_hot.astype(jnp.bfloat16), axis=1)
    combine = jnp.sum(
        jnp.where(slot_hot, gate_wts[:, :, None], jnp.zeros((), jnp.bfloat16)), axis=1
    )
    extra = 128
    seq_hot = (
        (jnp.arange(token_count, dtype=jnp.int32) // LEN)[:, None]
        == jnp.arange(extra, dtype=jnp.int32)[None, :]
    ).astype(jnp.bfloat16)
    payload = jnp.concatenate([tokens, seq_hot], axis=1)
    outgoing = lax.dot_general(
        placing, payload, (((0,), (0,)), ((), ())), preferred_element_type=jnp.float32
    )
    outgoing = jnp.concatenate(
        [outgoing[:, :model_width],
         lax.dot_general(combine, seq_hot, (((0,), (0,)), ((), ())),
                         preferred_element_type=jnp.float32)],
        axis=1,
    ).astype(jnp.bfloat16)
    outgoing = outgoing.reshape(experts, capacity, model_width + extra)
    arrived = lax.all_to_all(outgoing, "expert", split_axis=0, concat_axis=0, tiled=True)
    input_flat = arrived[:, :, :model_width].reshape(expert_size * capacity, model_width)
    my_meta = arrived[:, :, model_width:model_width + seq_count].astype(jnp.float32)
    same_src = jnp.eye(expert_size, dtype=jnp.float32)
    meta_t = jnp.transpose(my_meta, (2, 0, 1))
    sel_gate = same_src[:, None, :, None] * meta_t[None, :, :, :]
    sel_gate = sel_gate.reshape(row_seqs, expert_size * capacity)

    pre_act = jnp.dot(input_flat, weight_in[0], preferred_element_type=jnp.float32)
    gelu_val, slope_flat = gelu_parts(pre_act)
    hidden = gelu_val.astype(jnp.bfloat16)
    seq_hidden = jnp.dot(sel_gate.astype(jnp.bfloat16), hidden, preferred_element_type=jnp.float32)
    moe_seq = split_dot(seq_hidden, weight_out[0], (((1,), (0,)), ((), ())))
    moe_back = lax.all_to_all(
        moe_seq.reshape(expert_size, seq_count, model_width), "expert",
        split_axis=0, concat_axis=0, tiled=True,
    )
    moe_mine = jnp.sum(moe_back, axis=0)

    token_sum = jnp.sum(tokens.astype(jnp.float32).reshape(seq_count, LEN, model_width), axis=1)
    pooled = (token_sum + moe_mine) / LEN
    row_scale = lax.rsqrt(jnp.sum(pooled * pooled, axis=1) + EPSILON)
    unit_vec = pooled * row_scale[:, None]
    query_vec = unit_vec.astype(jnp.bfloat16)
    prem_count = premises.shape[0]
    key_rows = lax.all_gather(premises, "dp", axis=0, tiled=True)
    key_scale = lax.rsqrt(jnp.sum(jnp.square(key_rows.astype(jnp.float32)), axis=1) + EPSILON)
    key_index = jnp.arange(key_rows.shape[0], dtype=jnp.int32)
    own_positive = lax.dynamic_slice_in_dim(positive, device * seq_count, seq_count)
    mask_row = lax.dynamic_index_in_dim(tile_mask, device, 0, keepdims=False)
    key_open = jnp.repeat(mask_row, prem_count) == 1
    weighted_sum, partition, pos_vec = contrast_terms(
        query_vec,
        key_rows,
        key_scale,
        key_open[None, :],
        key_index[None, :] == own_positive[:, None],
    )
    delta_unit = LOSS_SCALE * SCORE_SCALE * (weighted_sum / partition[:, None] - pos_vec)
    delta_pooled = row_scale[:, None] * (
        delta_unit - unit_vec * jnp.sum(unit_vec * delta_unit, axis=1, keepdims=True)
    )
    delta_seq = (delta_pooled / LEN).astype(jnp.bfloat16)
    delta_row = lax.all_to_all(
        jnp.broadcast_to(delta_seq[None], (expert_size,) + delta_seq.shape), "expert",
        split_axis=0, concat_axis=0, tiled=True,
    ).reshape(row_seqs, model_width)

    dims_t = (((0,), (0,)), ((), ()))
    spread_t = lax.optimization_barrier(lax.dot_general(
        weight_out[0], delta_row, (((1,), (1,)), ((), ())), preferred_element_type=jnp.float32
    ).astype(jnp.bfloat16))
    spread_src = spread_t.T.astype(jnp.float32).reshape(expert_size, seq_count, ffn_width)
    dhidden = sum(
        my_meta[:, :, sl, None] * spread_src[:, None, sl, :] for sl in range(seq_count)
    ).reshape(expert_size * capacity, ffn_width)
    delta_pre = lax.optimization_barrier((dhidden * slope_flat).astype(jnp.bfloat16))
    grad_in_term = lax.dot_general(
        input_flat, delta_pre, dims_t, preferred_element_type=jnp.float32
    ).astype(jnp.bfloat16)
    grad_out_term = lax.dot_general(
        seq_hidden.astype(jnp.bfloat16), delta_row, dims_t, preferred_element_type=jnp.float32
    ).astype(jnp.bfloat16)
    grad_in, grad_out = reduce_scatter_2d(
        grad_in_term, grad_out_term, nx, ny, lax.rem(dp_index, nx), dp_index // nx
    )
    return (grad_in[None], grad_out[None])


def solution(mesh):
    in_specs = (
        P(("dp", "expert"), None),
        P(("dp", "expert"), None),
        P(),
        P("expert", None, None),
        P("expert", None, None),
        P("dp", None),
        P(),
        P(),
    )
    out_specs = (P("expert", "dp", None), P("expert", "dp", None))
    return jax.shard_map(
        on_device, mesh=mesh, in_specs=in_specs, out_specs=out_specs, check_vma=False
    )
```
